32 devices in a mesh: groups: 2 (over y), brick: 4 (over z), split: 2 (over x), sub: 2 (over core).
Axes of the slice: x: 2, y: 2, z: 4, core: 2. Of those that a mesh axis runs over, the one named last changes fastest.
Arguments:
- grad_out: bfloat16 [128, 32, 512], P(('groups', 'brick', 'split', 'sub')), parts along dimension 0, may hold values from -6 to 6
- features: bfloat16 [128, 32, 512], P(('groups', 'brick', 'split', 'sub')), parts along dimension 0, may hold values from -6 to 6
- kernel: bfloat16 [27, 32, 32], replicated, may hold values from -0.21875 to 0.21875
- block_count: int32 [32], P(('groups', 'brick', 'split', 'sub')), parts along dimension 0, may hold values from 1 to 4, as said below
- neighbours: int32 [128, 26], P(('groups', 'brick', 'split', 'sub')), parts along dimension 0, may hold values from 0 to 16, as said below
Outputs:
- grad_features: bfloat16 [128, 32, 512], P(('groups', 'brick', 'split', 'sub')), parts along dimension 0
- kernel_grad: float32 [54, 32, 32], P('groups'), parts along dimension 0
The draws below stay inside these ranges and needn't reach their ends.
There are 2 independent parts, one for each index of `groups`. The reference program is written for one: setup_inputs(seed, part) draws one part's arguments, and reference() takes and returns one part's arrays. A program takes and returns all parts, laid end to end along the dimension named above; an argument that names none is the same for every part. Nothing has to cross between parts.
Inputs may be any that keep to these rules, and one draw needn't show every extreme that they name: `block_count`: in every brick one device holds exactly 4 live blocks. `neighbours`: entry (q, k) is the slot, within the brick at block height offset c of direction k (periodic), of the active block at the neighbouring position (periodic in the first two dimensions), or 16 if that position is inactive; rows of slots that are not live hold 16; every active block has one slot.
All inputs are finite; a program needn't handle non-finite values.
Results may differ from the reference program's by a relative error of at most 0.001.
Values may be sent and summed in bfloat16 or wider, within the bound.
No kernel may reach another device: no remote copies, remote signals or barrier semaphores. Data moves between devices by JAX's collectives and lax.ppermute only.
A program may use at most 64 MiB of HBM per device.

```python
import math
import jax
import jax.numpy as jnp
from jax import lax

C = 32
BLK_DEV = 4
GY = 16
BLOCKS = 64
N_BRICK = 4
N_SPLIT = 2
N_SUB = 2


NEAR_DIRECTIONS = [(a, b, c) for a in (-1, 0, 1) for b in (-1, 0, 1) for c in (-1, 0, 1) if (a, b, c) != (0, 0, 0)]


def layout(key):
    folded = jax.random.fold_in(key, 7)
    k_count, k_full, k_perm = jax.random.split(folded, 3)
    per_brick = N_SPLIT * N_SUB
    slot_total = per_brick * BLK_DEV
    extent_x = 2 * per_brick * BLK_DEV // GY
    cell_total = extent_x * GY
    lowest = max(1, BLK_DEV // 8)
    counts = jax.random.randint(k_count, (N_BRICK, per_brick), lowest, BLK_DEV // 2 + 1)
    fullest = jax.random.randint(k_full, (N_BRICK, 1), 0, per_brick)
    counts = jnp.where(jnp.arange(per_brick)[None, :] == fullest, BLK_DEV, counts).astype(jnp.int32)
    orders = jax.vmap(lambda k: jax.random.permutation(k, cell_total))(jax.random.split(k_perm, N_BRICK))
    slot_ids = jnp.arange(slot_total, dtype=jnp.int32)
    live_slots = (slot_ids % BLK_DEV)[None, :] < jnp.repeat(counts, BLK_DEV, axis=1)
    cell_of = jnp.where(live_slots, orders[:, :slot_total], cell_total).astype(jnp.int32)
    brick_ids = jnp.arange(N_BRICK, dtype=jnp.int32)[:, None]
    cell_table = jnp.full((N_BRICK, cell_total + 1), slot_total, jnp.int32)
    cell_table = cell_table.at[jnp.broadcast_to(brick_ids, (N_BRICK, slot_total)), cell_of].set(jnp.broadcast_to(slot_ids, (N_BRICK, slot_total)))
    cell_table = cell_table[:, :cell_total]
    cell_x = cell_of // GY
    cell_y = cell_of % GY
    columns = []
    for a, b, c in NEAR_DIRECTIONS:
        near_brick = jnp.broadcast_to((brick_ids + c) % N_BRICK, (N_BRICK, slot_total))
        near_cell = (cell_x + a) % extent_x * GY + (cell_y + b) % GY
        found_slot = cell_table[near_brick, near_cell]
        columns.append(jnp.where(live_slots, found_slot, slot_total))
    linked = jnp.stack(columns, axis=-1).reshape(N_BRICK * slot_total, 26).astype(jnp.int32)
    return (counts.reshape(-1), linked)


def draw_block_count(key, part):
    return layout(key)[0]


def draw_neighbours(key, part):
    return layout(key)[1]


def block_levels(stream_key, dims, shards, smallest, high):
    level = 1.0
    for position, shards_of in shards:
        heights = jax.random.uniform(jax.random.fold_in(jax.random.fold_in(stream_key, 6), position), (shards_of,), jnp.float32, smallest / len(shards), high / len(shards))
        level = level * jnp.repeat(jnp.exp(heights), dims[position] // shards_of).reshape((-1,) + (1,) * (len(dims) - 1 - position))
    return level


def gaussian(rng, extent, width, bound, cuts=(), held_as=jnp.bfloat16):
    entries = jax.random.normal(rng, extent, jnp.float32) * width
    if len(cuts) > 0:
        entries = block_levels(rng, extent, cuts, -0.22, 0.18) * entries
    return jnp.clip(entries, min=-bound, max=bound).astype(held_as)


def setup_inputs(seed: int = 0, part: int = 0) -> dict:
    splits = jax.random.split(jax.random.key(seed), 6)
    own_keys = jax.random.split(jax.random.fold_in(splits[5], part), 6)
    return {
        "grad_out": gaussian(own_keys[0], (BLOCKS, C, 512), 1.0, 6.0, ((0, 16),)),
        "features": gaussian(own_keys[1], (BLOCKS, C, 512), 1.0, 6.0, ((0, 16),)),
        "kernel": gaussian(splits[2], (27, C, C), (27 * C) ** -0.5, 0.21875),
        "block_count": draw_block_count(jax.random.fold_in(jax.random.fold_in(splits[5], part), 71), part),
        "neighbours": draw_neighbours(jax.random.fold_in(jax.random.fold_in(splits[5], part), 71), part),
    }


DIRECTIONS = [(a, b, c) for a in (-1, 0, 1) for b in (-1, 0, 1) for c in (-1, 0, 1)]
NEIGHBOURS = [d for d in DIRECTIONS if d != (0, 0, 0)]

def window(offset):
    if offset < 0:
        return slice(7, 8)
    if offset > 0:
        return slice(0, 1)
    return slice(0, 8)

def assemble(pieces):
    planes = []
    for a in (-1, 0, 1):
        row_list = []
        for b in (-1, 0, 1):
            row_list.append(jnp.concatenate([pieces[a, b, c] for c in (-1, 0, 1)], axis=4))
        planes.append(jnp.concatenate(row_list, axis=3))
    return jnp.concatenate(planes, axis=2)

def contract(padded, source, kernel):
    blocks_here, channels = (source.shape[0], source.shape[1])
    input_grad = jnp.zeros((blocks_here, channels, 512), jnp.float32)
    weight_grads = {}
    for c in (-1, 0, 1):
        shifted = jnp.concatenate([padded[:, :, 1 - a:9 - a, 1 - b:9 - b, 1 - c:9 - c].reshape(blocks_here, channels, 512) for a in (-1, 0, 1) for b in (-1, 0, 1)], axis=1).astype(jnp.float32)
        offset_ids = [(a + 1) * 9 + (b + 1) * 3 + (c + 1) for a in (-1, 0, 1) for b in (-1, 0, 1)]
        stacked = jnp.stack([kernel[i] for i in offset_ids], axis=0)
        mixing = jnp.transpose(stacked, (1, 0, 2)).reshape(channels, 9 * channels).astype(jnp.float32)
        input_grad = input_grad + jnp.einsum('ik,bkv->biv', mixing, shifted)
        weight_part = jnp.einsum('biv,bkv->ik', source.astype(jnp.float32), shifted).reshape(channels, 9, channels)
        for j, i in enumerate(offset_ids):
            weight_grads[i] = weight_part[:, j]
    return (input_grad, jnp.stack([weight_grads[i] for i in range(27)], axis=0))

def reference(grad_out, features, kernel, block_count, neighbours):
    channels = grad_out.shape[1]
    slot_total = N_SPLIT * N_SUB * BLK_DEV
    cubes = grad_out.reshape(N_BRICK, slot_total, channels, 8, 8, 8)
    sources = features.reshape(N_BRICK, slot_total, channels, 512)
    lists = neighbours.reshape(N_BRICK, slot_total, 26)
    zero_block = jnp.zeros((1, channels, 8, 8, 8), grad_out.dtype)
    live_slots = (jnp.arange(slot_total) % BLK_DEV)[None, :] < jnp.repeat(block_count.reshape(N_BRICK, N_SPLIT * N_SUB), BLK_DEV, axis=1)

    def one_brick(running, brick_id):
        own = cubes[brick_id]
        tables = {-1: jnp.concatenate([cubes[(brick_id - 1) % N_BRICK], zero_block], axis=0), 0: jnp.concatenate([own, zero_block], axis=0), 1: jnp.concatenate([cubes[(brick_id + 1) % N_BRICK], zero_block], axis=0)}
        brick_list = lists[brick_id]
        pieces = {(0, 0, 0): own}
        for k, (a, b, c) in enumerate(NEIGHBOURS):
            fetched = jnp.take(tables[c], brick_list[:, k], axis=0)
            pieces[a, b, c] = fetched[:, :, window(a), window(b), window(c)]
        padded = assemble(pieces)
        live_mask = live_slots[brick_id][:, None, None]
        masked = jnp.where(live_mask, sources[brick_id], jnp.zeros_like(sources[brick_id]))
        input_grad, weight_grads = contract(padded, masked, kernel)
        grad_block = jnp.where(live_mask, input_grad, jnp.zeros_like(input_grad)).astype(jnp.bfloat16)
        return (running + weight_grads, grad_block)
    totals, grad_blocks = lax.scan(one_brick, jnp.zeros((27, channels, channels), jnp.float32), jnp.arange(N_BRICK))
    scaling = 1.0 / math.sqrt(N_BRICK * slot_total * 512)
    return (grad_blocks.reshape(N_BRICK * slot_total, channels, 512), totals * scaling)
```

```python
import math

import jax
import jax.numpy as jnp
from jax import lax
from jax.experimental import pallas as pl
from jax.experimental.pallas import tpu as pltpu
from jax.sharding import PartitionSpec as P

DIRECTIONS = [(a, b, c) for a in (-1, 0, 1) for b in (-1, 0, 1) for c in (-1, 0, 1)]
NEIGHBOURS = [d for d in DIRECTIONS if d != (0, 0, 0)]
VOX = 512


def from_behind(block, axis, distance):
    devices = range(lax.axis_size(axis))
    route = [((i - distance) % len(devices), i) for i in devices]
    return lax.ppermute(block, axis, route)


def butterfly_sum(x, axes):
    for axis in axes:
        n = lax.axis_size(axis)
        if n & (n - 1):
            x = lax.psum(x, axis)
            continue
        bit = 1
        while bit < n:
            x = x + lax.ppermute(x, axis, [(i, i ^ bit) for i in range(n)])
            bit *= 2
    return x


def sources_of(d):
    a, b, c = d
    found = []
    for ex in sorted({0, -a}):
        for ey in sorted({0, -b}):
            for ez in sorted({0, -c}):
                if (ex, ey, ez) != (0, 0, 0):
                    found.append((ex, ey, ez))
    return sorted(found, key=lambda e: sum(1 for t in e if t != 0))


def make_kernel(blocks, channels, slots):
    def kernel(nbr_ref, cnt_ref, g_ref, f_ref, gath_ref, kmix_ref, gf_ref, wg_ref,
               same_ref, lay_ref, stack_ref):
        lane = lax.broadcasted_iota(jnp.int32, (channels, VOX), 1)
        coord = (lane // 64, (lane // 8) % 8, lane % 8)

        def boundary(axis, sign):
            return coord[axis] == (7 if sign < 0 else 0)

        rows = lax.broadcasted_iota(jnp.int32, (64, VOX), 0)
        cols = lax.broadcasted_iota(jnp.int32, (64, VOX), 1)
        spread = (cols // 8 == rows).astype(jnp.bfloat16)
        same_ref[slots] = jnp.zeros((channels, VOX), jnp.bfloat16)
        lay_ref[0, slots] = jnp.zeros((channels, VOX), jnp.bfloat16)
        lay_ref[1, slots] = jnp.zeros((channels, VOX), jnp.bfloat16)

        def fill(q, carry):
            row = gath_ref[q]
            same_ref[q] = row[:, 0:VOX]
            for t in range(2):
                layer = row[:, VOX + 64 * t:VOX + 64 * (t + 1)]
                wide = jnp.dot(layer, spread, preferred_element_type=jnp.float32)
                lay_ref[t, q] = wide.astype(jnp.bfloat16)
            return carry

        lax.fori_loop(0, slots, fill, 0)

        gf_ref[...] = jnp.zeros_like(gf_ref)
        wg_ref[...] = jnp.zeros_like(wg_ref)

        def body(s, carry):
            own = g_ref[s].astype(jnp.float32)

            def neighbour(e):
                q = jnp.minimum(nbr_ref[s, NEIGHBOURS.index(e)], slots)
                if e[2] == 0:
                    return same_ref[q].astype(jnp.float32)
                return lay_ref[0 if e[2] < 0 else 1, q].astype(jnp.float32)

            for di, d in enumerate(DIRECTIONS):
                z = own
                for e in sources_of(d):
                    region = None
                    for axis in range(3):
                        if e[axis] != 0:
                            part = boundary(axis, e[axis])
                            region = part if region is None else (region & part)
                    z = jnp.where(region, neighbour(e), z)
                a, b, c = d
                if c != 0:
                    z = jnp.where(coord[2] == (0 if c > 0 else 7),
                                  pltpu.roll(z, (-7 * c) % VOX, 1),
                                  pltpu.roll(z, c % VOX, 1))
                if b != 0:
                    z = jnp.where(coord[1] == (0 if b > 0 else 7),
                                  pltpu.roll(z, (-56 * b) % VOX, 1),
                                  pltpu.roll(z, (8 * b) % VOX, 1))
                if a != 0:
                    z = pltpu.roll(z, (64 * a) % VOX, 1)
                stack_ref[di * channels:(di + 1) * channels, :] = z.astype(jnp.bfloat16)
            st = stack_ref[...]
            gf = jnp.dot(kmix_ref[...], st, preferred_element_type=jnp.float32)
            gf_ref[s] = gf.astype(jnp.bfloat16)
            wg_ref[...] += lax.dot_general(
                f_ref[s], st, (((1,), (1,)), ((), ())), preferred_element_type=jnp.float32
            )
            return carry

        lax.fori_loop(0, jnp.minimum(cnt_ref[0], blocks), body, 0)

    return kernel


def local_conv(neighbours, block_count, grad_out, features, gathered, kmix):
    blocks, channels = grad_out.shape[0], grad_out.shape[1]
    slots = gathered.shape[0]
    smem = pl.BlockSpec(memory_space=pltpu.SMEM)
    vmem = pl.BlockSpec(memory_space=pltpu.VMEM)
    return pl.pallas_call(
        make_kernel(blocks, channels, slots),
        out_shape=(
            jax.ShapeDtypeStruct((blocks, channels, VOX), jnp.bfloat16),
            jax.ShapeDtypeStruct((channels, 27 * channels), jnp.float32),
        ),
        in_specs=[smem, smem, vmem, vmem, vmem, vmem],
        out_specs=(vmem, vmem),
        scratch_shapes=[
            pltpu.VMEM((slots + 1, channels, VOX), jnp.bfloat16),
            pltpu.VMEM((2, slots + 1, channels, VOX), jnp.bfloat16),
            pltpu.VMEM((27 * channels, VOX), jnp.bfloat16),
        ],
    )(neighbours, block_count, grad_out, features, gathered, kmix)


def on_device(grad_out, features, kernel, block_count, neighbours):
    blocks, channels = grad_out.shape[0], grad_out.shape[1]
    cubes = grad_out.reshape(blocks, channels, 8, 8, 8)
    lowest = cubes[:, :, :, :, 0].reshape(blocks, channels, 64)
    highest = cubes[:, :, :, :, 7].reshape(blocks, channels, 64)
    from_below = from_behind(highest, "brick", 1)
    from_above = from_behind(lowest, "brick", -1)
    packed = jnp.concatenate([grad_out, from_below, from_above], axis=2)
    gathered = lax.all_gather(packed, ("split", "sub"), axis=0, tiled=True)
    kmix = jnp.transpose(kernel, (1, 0, 2)).reshape(channels, 27 * channels)
    grad_features, wg = local_conv(neighbours, block_count, grad_out, features, gathered, kmix)
    wg = butterfly_sum(wg, ("sub", "split", "brick"))
    scaling = 1.0 / math.sqrt(
        lax.axis_size("brick") * lax.axis_size("split") * lax.axis_size("sub") * blocks * VOX
    )
    totals = jnp.transpose(wg.reshape(channels, 27, channels), (1, 0, 2)) * scaling
    return (grad_features, totals)


def solution(mesh):
    placed = (
        P(("groups", "brick", "split", "sub"), None, None),
        P(("groups", "brick", "split", "sub"), None, None),
        P(),
        P(("groups", "brick", "split", "sub")),
        P(("groups", "brick", "split", "sub"), None),
    )
    return jax.shard_map(
        on_device,
        mesh=mesh,
        in_specs=placed,
        out_specs=(P(("groups", "brick", "split", "sub"), None, None), P("groups", None, None)),
        check_vma=False,
    )
```

```python
import math

import jax
import jax.numpy as jnp
from jax import lax
from jax.experimental import pallas as pl
from jax.experimental.pallas import tpu as pltpu
from jax.sharding import PartitionSpec as P

DIRECTIONS = [(a, b, c) for a in (-1, 0, 1) for b in (-1, 0, 1) for c in (-1, 0, 1)]
NEIGHBOURS = [d for d in DIRECTIONS if d != (0, 0, 0)]
VOX = 512


def from_behind(block, axis, distance):
    devices = range(lax.axis_size(axis))
    route = [((i - distance) % len(devices), i) for i in devices]
    return lax.ppermute(block, axis, route)


def butterfly_sum(x, axes):
    for axis in axes:
        n = lax.axis_size(axis)
        if n & (n - 1):
            x = lax.psum(x, axis)
            continue
        bit = 1
        while bit < n:
            x = x + lax.ppermute(x, axis, [(i, i ^ bit) for i in range(n)])
            bit *= 2
    return x


def sources_of(d):
    a, b, c = d
    found = []
    for ex in sorted({0, -a}):
        for ey in sorted({0, -b}):
            for ez in sorted({0, -c}):
                if (ex, ey, ez) != (0, 0, 0):
                    found.append((ex, ey, ez))
    return sorted(found, key=lambda e: sum(1 for t in e if t != 0))


def make_kernel(blocks, channels, slots):
    def kernel(nbr_ref, cnt_ref, g_ref, f_ref, gath_ref, kmix_ref, gf_ref, wg_ref,
               same_ref, lay_ref, stack_ref):
        lane = lax.broadcasted_iota(jnp.int32, (channels, VOX), 1)
        coord = (lane // 64, (lane // 8) % 8, lane % 8)

        def boundary(axis, sign):
            return coord[axis] == (7 if sign < 0 else 0)

        rows = lax.broadcasted_iota(jnp.int32, (64, VOX), 0)
        cols = lax.broadcasted_iota(jnp.int32, (64, VOX), 1)
        spread = (cols // 8 == rows).astype(jnp.bfloat16)
        same_ref[slots] = jnp.zeros((channels, VOX), jnp.bfloat16)
        lay_ref[0, slots] = jnp.zeros((channels, VOX), jnp.bfloat16)
        lay_ref[1, slots] = jnp.zeros((channels, VOX), jnp.bfloat16)

        def fill(q, carry):
            row = gath_ref[q]
            same_ref[q] = row[:, 0:VOX]
            for t in range(2):
                layer = row[:, VOX + 64 * t:VOX + 64 * (t + 1)]
                wide = jnp.dot(layer, spread, preferred_element_type=jnp.float32)
                lay_ref[t, q] = wide.astype(jnp.bfloat16)
            return carry

        lax.fori_loop(0, slots, fill, 0)

        gf_ref[...] = jnp.zeros_like(gf_ref)
        wg_ref[...] = jnp.zeros_like(wg_ref)

        def body(s, carry):
            own = g_ref[s]

            def neighbour(e):
                q = jnp.minimum(nbr_ref[s, NEIGHBOURS.index(e)], slots)
                if e[2] == 0:
                    return same_ref[q]
                return lay_ref[0 if e[2] < 0 else 1, q]

            for a in (-1, 0, 1):
                for b in (-1, 0, 1):
                    rx = boundary(0, -a) if a != 0 else None
                    ry = boundary(1, -b) if b != 0 else None
                    flat = own
                    if a != 0:
                        flat = jnp.where(rx, neighbour((-a, 0, 0)), flat)
                    if b != 0:
                        flat = jnp.where(ry, neighbour((0, -b, 0)), flat)
                    if a != 0 and b != 0:
                        flat = jnp.where(rx & ry, neighbour((-a, -b, 0)), flat)
                    for c in (-1, 0, 1):
                        z = flat
                        if c != 0:
                            y = neighbour((0, 0, -c))
                            if a != 0:
                                y = jnp.where(rx, neighbour((-a, 0, -c)), y)
                            if b != 0:
                                y = jnp.where(ry, neighbour((0, -b, -c)), y)
                            if a != 0 and b != 0:
                                y = jnp.where(rx & ry, neighbour((-a, -b, -c)), y)
                            z = jnp.where(boundary(2, -c), y, flat)
                        if c != 0:
                            z = jnp.where(coord[2] == (0 if c > 0 else 7),
                                          pltpu.roll(z, (-7 * c) % VOX, 1),
                                          pltpu.roll(z, c % VOX, 1))
                        if b != 0:
                            z = jnp.where(coord[1] == (0 if b > 0 else 7),
                                          pltpu.roll(z, (-56 * b) % VOX, 1),
                                          pltpu.roll(z, (8 * b) % VOX, 1))
                        if a != 0:
                            z = pltpu.roll(z, (64 * a) % VOX, 1)
                        di = 9 * (a + 1) + 3 * (b + 1) + (c + 1)
                        stack_ref[di * channels:(di + 1) * channels, :] = z
            st = stack_ref[...]
            gf = jnp.dot(kmix_ref[...], st, preferred_element_type=jnp.float32)
            gf_ref[s] = gf.astype(jnp.bfloat16)
            wg_ref[...] += lax.dot_general(
                f_ref[s], st, (((1,), (1,)), ((), ())), preferred_element_type=jnp.float32
            )
            return carry

        lax.fori_loop(0, jnp.minimum(cnt_ref[0], blocks), body, 0)

    return kernel


def local_conv(neighbours, block_count, grad_out, features, gathered, kmix):
    blocks, channels = grad_out.shape[0], grad_out.shape[1]
    slots = gathered.shape[0]
    smem = pl.BlockSpec(memory_space=pltpu.SMEM)
    vmem = pl.BlockSpec(memory_space=pltpu.VMEM)
    return pl.pallas_call(
        make_kernel(blocks, channels, slots),
        out_shape=(
            jax.ShapeDtypeStruct((blocks, channels, VOX), jnp.bfloat16),
            jax.ShapeDtypeStruct((channels, 27 * channels), jnp.float32),
        ),
        in_specs=[smem, smem, vmem, vmem, vmem, vmem],
        out_specs=(vmem, vmem),
        scratch_shapes=[
            pltpu.VMEM((slots + 1, channels, VOX), jnp.bfloat16),
            pltpu.VMEM((2, slots + 1, channels, VOX), jnp.bfloat16),
            pltpu.VMEM((27 * channels, VOX), jnp.bfloat16),
        ],
    )(neighbours, block_count, grad_out, features, gathered, kmix)


def on_device(grad_out, features, kernel, block_count, neighbours):
    blocks, channels = grad_out.shape[0], grad_out.shape[1]
    cubes = grad_out.reshape(blocks, channels, 8, 8, 8)
    lowest = cubes[:, :, :, :, 0].reshape(blocks, channels, 64)
    highest = cubes[:, :, :, :, 7].reshape(blocks, channels, 64)
    from_below = from_behind(highest, "brick", 1)
    from_above = from_behind(lowest, "brick", -1)
    packed = jnp.concatenate([grad_out, from_below, from_above], axis=2)
    gathered = lax.all_gather(packed, ("split", "sub"), axis=0, tiled=True)
    kmix = jnp.transpose(kernel, (1, 0, 2)).reshape(channels, 27 * channels)
    grad_features, wg = local_conv(neighbours, block_count, grad_out, features, gathered, kmix)
    wg = butterfly_sum(wg, ("sub", "split", "brick"))
    scaling = 1.0 / math.sqrt(
        lax.axis_size("brick") * lax.axis_size("split") * lax.axis_size("sub") * blocks * VOX
    )
    totals = jnp.transpose(wg.reshape(channels, 27, channels), (1, 0, 2)) * scaling
    return (grad_features, totals)


def solution(mesh):
    placed = (
        P(("groups", "brick", "split", "sub"), None, None),
        P(("groups", "brick", "split", "sub"), None, None),
        P(),
        P(("groups", "brick", "split", "sub")),
        P(("groups", "brick", "split", "sub"), None),
    )
    return jax.shard_map(
        on_device,
        mesh=mesh,
        in_specs=placed,
        out_specs=(P(("groups", "brick", "split", "sub"), None, None), P("groups", None, None)),
        check_vma=False,
    )
```

```python
import math

import jax
import jax.numpy as jnp
from jax import lax
from jax.experimental import pallas as pl
from jax.experimental.pallas import tpu as pltpu
from jax.sharding import PartitionSpec as P

DIRECTIONS = [(a, b, c) for a in (-1, 0, 1) for b in (-1, 0, 1) for c in (-1, 0, 1)]
NEIGHBOURS = [d for d in DIRECTIONS if d != (0, 0, 0)]
VOX = 512


def from_behind(block, axis, distance):
    devices = range(lax.axis_size(axis))
    route = [((i - distance) % len(devices), i) for i in devices]
    return lax.ppermute(block, axis, route)


def butterfly_sum(x, axes):
    for axis in axes:
        n = lax.axis_size(axis)
        if n & (n - 1):
            x = lax.psum(x, axis)
            continue
        bit = 1
        while bit < n:
            x = x + lax.ppermute(x, axis, [(i, i ^ bit) for i in range(n)])
            bit *= 2
    return x


def sources_of(d):
    a, b, c = d
    found = []
    for ex in sorted({0, -a}):
        for ey in sorted({0, -b}):
            for ez in sorted({0, -c}):
                if (ex, ey, ez) != (0, 0, 0):
                    found.append((ex, ey, ez))
    return sorted(found, key=lambda e: sum(1 for t in e if t != 0))


def make_kernel(blocks, channels, peers):
    slots = blocks * peers

    def kernel(nbr_ref, cnt_ref, me_ref, g_ref, f_ref, kmix_ref, *rest):
        recv_refs = rest[:peers]
        gf_ref, wg_ref, same_ref, lay_ref, stack_ref = rest[peers:]
        lane = lax.broadcasted_iota(jnp.int32, (channels, VOX), 1)
        coord = (lane // 64, (lane // 8) % 8, lane % 8)

        def boundary(axis, sign):
            return coord[axis] == (7 if sign < 0 else 0)

        rows = lax.broadcasted_iota(jnp.int32, (64, VOX), 0)
        cols = lax.broadcasted_iota(jnp.int32, (64, VOX), 1)
        spread = (cols // 8 == rows).astype(jnp.bfloat16)
        same_ref[slots] = jnp.zeros((channels, VOX), jnp.bfloat16)
        lay_ref[0, slots] = jnp.zeros((channels, VOX), jnp.bfloat16)
        lay_ref[1, slots] = jnp.zeros((channels, VOX), jnp.bfloat16)

        for k in range(peers):
            def fill(s, carry, k=k):
                row = recv_refs[k][s]
                q = (jnp.bitwise_xor(me_ref[0], k)) * blocks + s
                same_ref[q] = row[:, 0:VOX]
                for t in range(2):
                    layer = row[:, VOX + 64 * t:VOX + 64 * (t + 1)]
                    wide = jnp.dot(layer, spread, preferred_element_type=jnp.float32)
                    lay_ref[t, q] = wide.astype(jnp.bfloat16)
                return carry

            lax.fori_loop(0, blocks, fill, 0)

        gf_ref[...] = jnp.zeros_like(gf_ref)
        wg_ref[...] = jnp.zeros_like(wg_ref)

        def body(s, carry):
            own = g_ref[s]

            def neighbour(e):
                q = jnp.minimum(nbr_ref[s, NEIGHBOURS.index(e)], slots)
                if e[2] == 0:
                    return same_ref[q]
                return lay_ref[0 if e[2] < 0 else 1, q]

            for a in (-1, 0, 1):
                for b in (-1, 0, 1):
                    rx = boundary(0, -a) if a != 0 else None
                    ry = boundary(1, -b) if b != 0 else None
                    flat = own
                    if a != 0:
                        flat = jnp.where(rx, neighbour((-a, 0, 0)), flat)
                    if b != 0:
                        flat = jnp.where(ry, neighbour((0, -b, 0)), flat)
                    if a != 0 and b != 0:
                        flat = jnp.where(rx & ry, neighbour((-a, -b, 0)), flat)
                    for c in (-1, 0, 1):
                        z = flat
                        if c != 0:
                            y = neighbour((0, 0, -c))
                            if a != 0:
                                y = jnp.where(rx, neighbour((-a, 0, -c)), y)
                            if b != 0:
                                y = jnp.where(ry, neighbour((0, -b, -c)), y)
                            if a != 0 and b != 0:
                                y = jnp.where(rx & ry, neighbour((-a, -b, -c)), y)
                            z = jnp.where(boundary(2, -c), y, flat)
                        if c != 0:
                            z = jnp.where(coord[2] == (0 if c > 0 else 7),
                                          pltpu.roll(z, (-7 * c) % VOX, 1),
                                          pltpu.roll(z, c % VOX, 1))
                        if b != 0:
                            z = jnp.where(coord[1] == (0 if b > 0 else 7),
                                          pltpu.roll(z, (-56 * b) % VOX, 1),
                                          pltpu.roll(z, (8 * b) % VOX, 1))
                        if a != 0:
                            z = pltpu.roll(z, (64 * a) % VOX, 1)
                        di = 9 * (a + 1) + 3 * (b + 1) + (c + 1)
                        stack_ref[di * channels:(di + 1) * channels, :] = z
            st = stack_ref[...]
            gf = jnp.dot(kmix_ref[...], st, preferred_element_type=jnp.float32)
            gf_ref[s] = gf.astype(jnp.bfloat16)
            wg_ref[...] += lax.dot_general(
                f_ref[s], st, (((1,), (1,)), ((), ())), preferred_element_type=jnp.float32
            )
            return carry

        lax.fori_loop(0, jnp.minimum(cnt_ref[0], blocks), body, 0)

    return kernel


def local_conv(neighbours, block_count, me, grad_out, features, kmix, received):
    blocks, channels = grad_out.shape[0], grad_out.shape[1]
    peers = len(received)
    slots = blocks * peers
    smem = pl.BlockSpec(memory_space=pltpu.SMEM)
    vmem = pl.BlockSpec(memory_space=pltpu.VMEM)
    return pl.pallas_call(
        make_kernel(blocks, channels, peers),
        out_shape=(
            jax.ShapeDtypeStruct((blocks, channels, VOX), jnp.bfloat16),
            jax.ShapeDtypeStruct((channels, 27 * channels), jnp.float32),
        ),
        in_specs=[smem, smem, smem, vmem, vmem, vmem] + [vmem] * peers,
        out_specs=(vmem, vmem),
        scratch_shapes=[
            pltpu.VMEM((slots + 1, channels, VOX), jnp.bfloat16),
            pltpu.VMEM((2, slots + 1, channels, VOX), jnp.bfloat16),
            pltpu.VMEM((27 * channels, VOX), jnp.bfloat16),
        ],
    )(neighbours, block_count, me, grad_out, features, kmix, *received)


def on_device(grad_out, features, kernel, block_count, neighbours):
    blocks, channels = grad_out.shape[0], grad_out.shape[1]
    cubes = grad_out.reshape(blocks, channels, 8, 8, 8)
    lowest = cubes[:, :, :, :, 0].reshape(blocks, channels, 64)
    highest = cubes[:, :, :, :, 7].reshape(blocks, channels, 64)
    from_below = from_behind(highest, "brick", 1)
    from_above = from_behind(lowest, "brick", -1)
    packed = jnp.concatenate([grad_out, from_below, from_above], axis=2)
    peers = lax.axis_size("split") * lax.axis_size("sub")
    assert peers & (peers - 1) == 0
    received = [packed] + [
        lax.ppermute(packed, ("split", "sub"), [(i, i ^ k) for i in range(peers)])
        for k in range(1, peers)
    ]
    me = (lax.axis_index("split") * lax.axis_size("sub") + lax.axis_index("sub")).astype(jnp.int32)
    kmix = jnp.transpose(kernel, (1, 0, 2)).reshape(channels, 27 * channels)
    grad_features, wg = local_conv(
        neighbours, block_count, me.reshape(1), grad_out, features, kmix, received
    )
    wg = butterfly_sum(wg, ("sub", "split", "brick"))
    scaling = 1.0 / math.sqrt(
        lax.axis_size("brick") * lax.axis_size("split") * lax.axis_size("sub") * blocks * VOX
    )
    totals = jnp.transpose(wg.reshape(channels, 27, channels), (1, 0, 2)) * scaling
    return (grad_features, totals)


def solution(mesh):
    placed = (
        P(("groups", "brick", "split", "sub"), None, None),
        P(("groups", "brick", "split", "sub"), None, None),
        P(),
        P(("groups", "brick", "split", "sub")),
        P(("groups", "brick", "split", "sub"), None),
    )
    return jax.shard_map(
        on_device,
        mesh=mesh,
        in_specs=placed,
        out_specs=(P(("groups", "brick", "split", "sub"), None, None), P("groups", None, None)),
        check_vma=False,
    )
```

```python
import math

import jax
import jax.numpy as jnp
from jax import lax
from jax.experimental import pallas as pl
from jax.experimental.pallas import tpu as pltpu
from jax.sharding import PartitionSpec as P

DIRECTIONS = [(a, b, c) for a in (-1, 0, 1) for b in (-1, 0, 1) for c in (-1, 0, 1)]
NEIGHBOURS = [d for d in DIRECTIONS if d != (0, 0, 0)]
VOX = 512


def from_behind(block, axis, distance):
    devices = range(lax.axis_size(axis))
    route = [((i - distance) % len(devices), i) for i in devices]
    return lax.ppermute(block, axis, route)


def butterfly_sum(x, axes):
    for axis in axes:
        n = lax.axis_size(axis)
        if n & (n - 1):
            x = lax.psum(x, axis)
            continue
        bit = 1
        while bit < n:
            x = x + lax.ppermute(x, axis, [(i, i ^ bit) for i in range(n)])
            bit *= 2
    return x


def sources_of(d):
    a, b, c = d
    found = []
    for ex in sorted({0, -a}):
        for ey in sorted({0, -b}):
            for ez in sorted({0, -c}):
                if (ex, ey, ez) != (0, 0, 0):
                    found.append((ex, ey, ez))
    return sorted(found, key=lambda e: sum(1 for t in e if t != 0))


def face_selector(rows, cols, transpose):
    v, j = (cols, rows) if transpose else (rows, cols)
    face, r = j // 64, j % 64
    hi, lo = r // 8, r % 8
    target = jnp.where(face == 0, r, 448 + r)
    target = jnp.where(face == 2, hi * 64 + lo, target)
    target = jnp.where(face == 3, hi * 64 + 56 + lo, target)
    hit = v == target
    if transpose:
        inner = (v // 64 != 0) & (v // 64 != 7)
        hit = hit & ((face < 2) | inner)
    return hit.astype(jnp.bfloat16)


def pack_kernel(g_ref, faces_ref, low_ref, high_ref):
    rows = lax.broadcasted_iota(jnp.int32, (VOX, 256), 0)
    cols = lax.broadcasted_iota(jnp.int32, (VOX, 256), 1)
    pick = face_selector(rows, cols, False)
    lrows = lax.broadcasted_iota(jnp.int32, (VOX, 128), 0)
    lcols = lax.broadcasted_iota(jnp.int32, (VOX, 128), 1)
    layer_pick = (lrows == (lcols % 64) * 8 + 7 * (lcols // 64)).astype(jnp.bfloat16)
    for s in range(g_ref.shape[0]):
        g = g_ref[s]
        faces_ref[s] = jnp.dot(g, pick, preferred_element_type=jnp.float32).astype(jnp.bfloat16)
        layers = jnp.dot(g, layer_pick, preferred_element_type=jnp.float32).astype(jnp.bfloat16)
        low_ref[s] = layers[:, 0:64]
        high_ref[s] = layers[:, 64:128]


def pack(grad_out):
    blocks, channels = grad_out.shape[0], grad_out.shape[1]
    vmem = pl.BlockSpec(memory_space=pltpu.VMEM)
    return pl.pallas_call(
        pack_kernel,
        out_shape=(
            jax.ShapeDtypeStruct((blocks, channels, 256), jnp.bfloat16),
            jax.ShapeDtypeStruct((blocks, channels, 64), jnp.bfloat16),
            jax.ShapeDtypeStruct((blocks, channels, 64), jnp.bfloat16),
        ),
        in_specs=[vmem],
        out_specs=(vmem, vmem, vmem),
    )(grad_out)


def make_kernel(blocks, channels, peers, scaling):
    slots = blocks * peers

    def kernel(nbr_ref, cnt_ref, me_ref, g_ref, f_ref, kmix_ref, *rest):
        face_refs = rest[:peers]
        layer_refs = rest[peers:2 * peers]
        gf_ref, wg_ref, same_ref, lay_ref, stack_ref, acc_ref = rest[2 * peers:]
        lane = lax.broadcasted_iota(jnp.int32, (channels, VOX), 1)
        coord = (lane // 64, (lane // 8) % 8, lane % 8)

        def boundary(axis, sign):
            return coord[axis] == (7 if sign < 0 else 0)

        rows = lax.broadcasted_iota(jnp.int32, (64, VOX), 0)
        cols = lax.broadcasted_iota(jnp.int32, (64, VOX), 1)
        spread = (cols // 8 == rows).astype(jnp.bfloat16)
        same_ref[slots] = jnp.zeros((channels, VOX), jnp.bfloat16)
        lay_ref[0, slots] = jnp.zeros((channels, VOX), jnp.bfloat16)
        lay_ref[1, slots] = jnp.zeros((channels, VOX), jnp.bfloat16)

        place = face_selector(
            lax.broadcasted_iota(jnp.int32, (256, VOX), 0),
            lax.broadcasted_iota(jnp.int32, (256, VOX), 1),
            True,
        )
        for k in range(peers):
            def fill(s, carry, k=k):
                q = (jnp.bitwise_xor(me_ref[0], k)) * blocks + s
                wide = jnp.dot(face_refs[k][s], place, preferred_element_type=jnp.float32)
                same_ref[q] = wide.astype(jnp.bfloat16)
                row = layer_refs[k][s]
                for t in range(2):
                    layer = row[:, 64 * t:64 * (t + 1)]
                    wide = jnp.dot(layer, spread, preferred_element_type=jnp.float32)
                    lay_ref[t, q] = wide.astype(jnp.bfloat16)
                return carry

            lax.fori_loop(0, blocks, fill, 0)

        gf_ref[...] = jnp.zeros_like(gf_ref)
        acc_ref[...] = jnp.zeros_like(acc_ref)

        def body(s, carry):
            own = g_ref[s]

            def neighbour(e):
                q = jnp.minimum(nbr_ref[s, NEIGHBOURS.index(e)], slots)
                if e[2] == 0:
                    return same_ref[q]
                return lay_ref[0 if e[2] < 0 else 1, q]

            for a in (-1, 0, 1):
                for b in (-1, 0, 1):
                    rx = boundary(0, -a) if a != 0 else None
                    ry = boundary(1, -b) if b != 0 else None
                    flat = own
                    if a != 0:
                        flat = jnp.where(rx, neighbour((-a, 0, 0)), flat)
                    if b != 0:
                        flat = jnp.where(ry, neighbour((0, -b, 0)), flat)
                    if a != 0 and b != 0:
                        flat = jnp.where(rx & ry, neighbour((-a, -b, 0)), flat)
                    for c in (-1, 0, 1):
                        z = flat
                        if c != 0:
                            y = neighbour((0, 0, -c))
                            if a != 0:
                                y = jnp.where(rx, neighbour((-a, 0, -c)), y)
                            if b != 0:
                                y = jnp.where(ry, neighbour((0, -b, -c)), y)
                            if a != 0 and b != 0:
                                y = jnp.where(rx & ry, neighbour((-a, -b, -c)), y)
                            z = jnp.where(boundary(2, -c), y, flat)
                        if c != 0:
                            z = jnp.where(coord[2] == (0 if c > 0 else 7),
                                          pltpu.roll(z, (-7 * c) % VOX, 1),
                                          pltpu.roll(z, c % VOX, 1))
                        if b != 0:
                            z = jnp.where(coord[1] == (0 if b > 0 else 7),
                                          pltpu.roll(z, (-56 * b) % VOX, 1),
                                          pltpu.roll(z, (8 * b) % VOX, 1))
                        if a != 0:
                            z = pltpu.roll(z, (64 * a) % VOX, 1)
                        di = 9 * (a + 1) + 3 * (b + 1) + (c + 1)
                        stack_ref[di * channels:(di + 1) * channels, :] = z
            st = stack_ref[...]
            gf = jnp.dot(kmix_ref[...], st, preferred_element_type=jnp.float32)
            gf_ref[s] = gf.astype(jnp.bfloat16)
            acc_ref[...] += lax.dot_general(
                f_ref[s], st, (((1,), (1,)), ((), ())), preferred_element_type=jnp.float32
            )
            return carry

        lax.fori_loop(0, jnp.minimum(cnt_ref[0], blocks), body, 0)
        for d in range(27):
            wg_ref[d] = acc_ref[:, d * channels:(d + 1) * channels] * scaling

    return kernel


def local_conv(neighbours, block_count, me, grad_out, features, kmix, faces, layers, scaling):
    blocks, channels = grad_out.shape[0], grad_out.shape[1]
    peers = len(faces)
    slots = blocks * peers
    smem = pl.BlockSpec(memory_space=pltpu.SMEM)
    vmem = pl.BlockSpec(memory_space=pltpu.VMEM)
    return pl.pallas_call(
        make_kernel(blocks, channels, peers, scaling),
        out_shape=(
            jax.ShapeDtypeStruct((blocks, channels, VOX), jnp.bfloat16),
            jax.ShapeDtypeStruct((27, channels, channels), jnp.float32),
        ),
        in_specs=[smem, smem, smem, vmem, vmem, vmem] + [vmem] * (2 * peers),
        out_specs=(vmem, vmem),
        scratch_shapes=[
            pltpu.VMEM((slots + 1, channels, VOX), jnp.bfloat16),
            pltpu.VMEM((2, slots + 1, channels, VOX), jnp.bfloat16),
            pltpu.VMEM((27 * channels, VOX), jnp.bfloat16),
            pltpu.VMEM((channels, 27 * channels), jnp.float32),
        ],
    )(neighbours, block_count, me, grad_out, features, kmix, *faces, *layers)


def on_device(grad_out, features, kernel, block_count, neighbours):
    blocks, channels = grad_out.shape[0], grad_out.shape[1]
    faces, lowest, highest = pack(grad_out)
    peers = lax.axis_size("split") * lax.axis_size("sub")
    assert peers & (peers - 1) == 0

    def spread_in_brick(x):
        return [x] + [
            lax.ppermute(x, ("split", "sub"), [(i, i ^ k) for i in range(peers)])
            for k in range(1, peers)
        ]

    from_below = from_behind(highest, "brick", 1)
    from_above = from_behind(lowest, "brick", -1)
    all_faces = spread_in_brick(faces)
    all_layers = spread_in_brick(jnp.concatenate([from_below, from_above], axis=2))
    me = (lax.axis_index("split") * lax.axis_size("sub") + lax.axis_index("sub")).astype(jnp.int32)
    kmix = jnp.transpose(kernel, (1, 0, 2)).reshape(channels, 27 * channels)
    scaling = 1.0 / math.sqrt(
        lax.axis_size("brick") * lax.axis_size("split") * lax.axis_size("sub") * blocks * VOX
    )
    grad_features, wg = local_conv(
        neighbours, block_count, me.reshape(1), grad_out, features, kmix,
        all_faces, all_layers, scaling,
    )
    totals = butterfly_sum(wg, ("sub", "split", "brick"))
    return (grad_features, totals)


def solution(mesh):
    placed = (
        P(("groups", "brick", "split", "sub"), None, None),
        P(("groups", "brick", "split", "sub"), None, None),
        P(),
        P(("groups", "brick", "split", "sub")),
        P(("groups", "brick", "split", "sub"), None),
    )
    return jax.shard_map(
        on_device,
        mesh=mesh,
        in_specs=placed,
        out_specs=(P(("groups", "brick", "split", "sub"), None, None), P("groups", None, None)),
        check_vma=False,
    )
```

```python
import math

import jax
import jax.numpy as jnp
from jax import lax
from jax.experimental import pallas as pl
from jax.experimental.pallas import tpu as pltpu
from jax.sharding import PartitionSpec as P

DIRECTIONS = [(a, b, c) for a in (-1, 0, 1) for b in (-1, 0, 1) for c in (-1, 0, 1)]
NEIGHBOURS = [d for d in DIRECTIONS if d != (0, 0, 0)]
VOX = 512


def from_behind(block, axis, distance):
    devices = range(lax.axis_size(axis))
    route = [((i - distance) % len(devices), i) for i in devices]
    return lax.ppermute(block, axis, route)


def butterfly_sum(x, axes):
    for axis in axes:
        n = lax.axis_size(axis)
        if n & (n - 1):
            x = lax.psum(x, axis)
            continue
        bit = 1
        while bit < n:
            x = x + lax.ppermute(x, axis, [(i, i ^ bit) for i in range(n)])
            bit *= 2
    return x


def sources_of(d):
    a, b, c = d
    found = []
    for ex in sorted({0, -a}):
        for ey in sorted({0, -b}):
            for ez in sorted({0, -c}):
                if (ex, ey, ez) != (0, 0, 0):
                    found.append((ex, ey, ez))
    return sorted(found, key=lambda e: sum(1 for t in e if t != 0))


def face_selector(rows, cols, transpose):
    v, j = (cols, rows) if transpose else (rows, cols)
    face, r = j // 64, j % 64
    hi, lo = r // 8, r % 8
    target = jnp.where(face == 0, r, 448 + r)
    target = jnp.where(face == 2, hi * 64 + lo, target)
    target = jnp.where(face == 3, hi * 64 + 56 + lo, target)
    hit = v == target
    if transpose:
        inner = (v // 64 != 0) & (v // 64 != 7)
        hit = hit & ((face < 2) | inner)
    return hit.astype(jnp.bfloat16)


def pack_kernel(g_ref, faces_ref, low_ref, high_ref):
    rows = lax.broadcasted_iota(jnp.int32, (VOX, 256), 0)
    cols = lax.broadcasted_iota(jnp.int32, (VOX, 256), 1)
    pick = face_selector(rows, cols, False)
    lrows = lax.broadcasted_iota(jnp.int32, (VOX, 128), 0)
    lcols = lax.broadcasted_iota(jnp.int32, (VOX, 128), 1)
    layer_pick = (lrows == (lcols % 64) * 8 + 7 * (lcols // 64)).astype(jnp.bfloat16)
    for s in range(g_ref.shape[0]):
        g = g_ref[s]
        faces_ref[s] = jnp.dot(g, pick, preferred_element_type=jnp.float32).astype(jnp.bfloat16)
        layers = jnp.dot(g, layer_pick, preferred_element_type=jnp.float32).astype(jnp.bfloat16)
        low_ref[s] = layers[:, 0:64]
        high_ref[s] = layers[:, 64:128]


def pack(grad_out):
    blocks, channels = grad_out.shape[0], grad_out.shape[1]
    vmem = pl.BlockSpec(memory_space=pltpu.VMEM)
    return pl.pallas_call(
        pack_kernel,
        out_shape=(
            jax.ShapeDtypeStruct((blocks, channels, 256), jnp.bfloat16),
            jax.ShapeDtypeStruct((blocks, channels, 64), jnp.bfloat16),
            jax.ShapeDtypeStruct((blocks, channels, 64), jnp.bfloat16),
        ),
        in_specs=[vmem],
        out_specs=(vmem, vmem, vmem),
    )(grad_out)


def make_kernel(blocks, channels, peers, scaling):
    slots = blocks * peers

    def kernel(nbr_ref, cnt_ref, me_ref, g_ref, f_ref, kmix_ref, *rest):
        shared_refs = rest[:peers]
        gf_ref, wg_ref, same_ref, lay_ref, stack_ref, acc_ref = rest[peers:]
        lane = lax.broadcasted_iota(jnp.int32, (channels, VOX), 1)
        coord = (lane // 64, (lane // 8) % 8, lane % 8)

        def boundary(axis, sign):
            return coord[axis] == (7 if sign < 0 else 0)

        rows = lax.broadcasted_iota(jnp.int32, (64, VOX), 0)
        cols = lax.broadcasted_iota(jnp.int32, (64, VOX), 1)
        spread = (cols // 8 == rows).astype(jnp.bfloat16)
        same_ref[slots] = jnp.zeros((channels, VOX), jnp.bfloat16)
        lay_ref[0, slots] = jnp.zeros((channels, VOX), jnp.bfloat16)
        lay_ref[1, slots] = jnp.zeros((channels, VOX), jnp.bfloat16)

        place = face_selector(
            lax.broadcasted_iota(jnp.int32, (256, VOX), 0),
            lax.broadcasted_iota(jnp.int32, (256, VOX), 1),
            True,
        )
        for k in range(peers):
            def fill(s, carry, k=k):
                q = (jnp.bitwise_xor(me_ref[0], k)) * blocks + s
                row = shared_refs[k][s]
                wide = jnp.dot(row[:, 0:256], place, preferred_element_type=jnp.float32)
                same_ref[q] = wide.astype(jnp.bfloat16)
                for t in range(2):
                    layer = row[:, 256 + 64 * t:256 + 64 * (t + 1)]
                    wide = jnp.dot(layer, spread, preferred_element_type=jnp.float32)
                    lay_ref[t, q] = wide.astype(jnp.bfloat16)
                return carry

            lax.fori_loop(0, blocks, fill, 0)

        gf_ref[...] = jnp.zeros_like(gf_ref)
        acc_ref[...] = jnp.zeros_like(acc_ref)

        def body(s, carry):
            own = g_ref[s]

            def neighbour(e):
                q = jnp.minimum(nbr_ref[s, NEIGHBOURS.index(e)], slots)
                if e[2] == 0:
                    return same_ref[q]
                return lay_ref[0 if e[2] < 0 else 1, q]

            for a in (-1, 0, 1):
                for b in (-1, 0, 1):
                    rx = boundary(0, -a) if a != 0 else None
                    ry = boundary(1, -b) if b != 0 else None
                    flat = own
                    if a != 0:
                        flat = jnp.where(rx, neighbour((-a, 0, 0)), flat)
                    if b != 0:
                        flat = jnp.where(ry, neighbour((0, -b, 0)), flat)
                    if a != 0 and b != 0:
                        flat = jnp.where(rx & ry, neighbour((-a, -b, 0)), flat)
                    for c in (-1, 0, 1):
                        z = flat
                        if c != 0:
                            y = neighbour((0, 0, -c))
                            if a != 0:
                                y = jnp.where(rx, neighbour((-a, 0, -c)), y)
                            if b != 0:
                                y = jnp.where(ry, neighbour((0, -b, -c)), y)
                            if a != 0 and b != 0:
                                y = jnp.where(rx & ry, neighbour((-a, -b, -c)), y)
                            z = jnp.where(boundary(2, -c), y, flat)
                        if c != 0:
                            z = jnp.where(coord[2] == (0 if c > 0 else 7),
                                          pltpu.roll(z, (-7 * c) % VOX, 1),
                                          pltpu.roll(z, c % VOX, 1))
                        if b != 0:
                            z = jnp.where(coord[1] == (0 if b > 0 else 7),
                                          pltpu.roll(z, (-56 * b) % VOX, 1),
                                          pltpu.roll(z, (8 * b) % VOX, 1))
                        if a != 0:
                            z = pltpu.roll(z, (64 * a) % VOX, 1)
                        di = 9 * (a + 1) + 3 * (b + 1) + (c + 1)
                        stack_ref[di * channels:(di + 1) * channels, :] = z
            st = stack_ref[...]
            gf = jnp.dot(kmix_ref[...], st, preferred_element_type=jnp.float32)
            gf_ref[s] = gf.astype(jnp.bfloat16)
            acc_ref[...] += lax.dot_general(
                f_ref[s], st, (((1,), (1,)), ((), ())), preferred_element_type=jnp.float32
            )
            return carry

        lax.fori_loop(0, jnp.minimum(cnt_ref[0], blocks), body, 0)
        wg_ref[...] = acc_ref[...] * scaling

    return kernel


def local_conv(neighbours, block_count, me, grad_out, features, kmix, shared, scaling):
    blocks, channels = grad_out.shape[0], grad_out.shape[1]
    peers = len(shared)
    slots = blocks * peers
    smem = pl.BlockSpec(memory_space=pltpu.SMEM)
    vmem = pl.BlockSpec(memory_space=pltpu.VMEM)
    return pl.pallas_call(
        make_kernel(blocks, channels, peers, scaling),
        out_shape=(
            jax.ShapeDtypeStruct((blocks, channels, VOX), jnp.bfloat16),
            jax.ShapeDtypeStruct((channels, 27 * channels), jnp.float32),
        ),
        in_specs=[smem, smem, smem, vmem, vmem, vmem] + [vmem] * peers,
        out_specs=(vmem, vmem),
        scratch_shapes=[
            pltpu.VMEM((slots + 1, channels, VOX), jnp.bfloat16),
            pltpu.VMEM((2, slots + 1, channels, VOX), jnp.bfloat16),
            pltpu.VMEM((27 * channels, VOX), jnp.bfloat16),
            pltpu.VMEM((channels, 27 * channels), jnp.float32),
        ],
    )(neighbours, block_count, me, grad_out, features, kmix, *shared)


def on_device(grad_out, features, kernel, block_count, neighbours):
    blocks, channels = grad_out.shape[0], grad_out.shape[1]
    faces, lowest, highest = pack(grad_out)
    peers = lax.axis_size("split") * lax.axis_size("sub")
    assert peers & (peers - 1) == 0

    def spread_in_brick(x):
        return [x] + [
            lax.ppermute(x, ("split", "sub"), [(i, i ^ k) for i in range(peers)])
            for k in range(1, peers)
        ]

    from_below = from_behind(highest, "brick", 1)
    from_above = from_behind(lowest, "brick", -1)
    shared = spread_in_brick(jnp.concatenate([faces, from_below, from_above], axis=2))
    me = (lax.axis_index("split") * lax.axis_size("sub") + lax.axis_index("sub")).astype(jnp.int32)
    kmix = jnp.transpose(kernel, (1, 0, 2)).reshape(channels, 27 * channels)
    scaling = 1.0 / math.sqrt(
        lax.axis_size("brick") * lax.axis_size("split") * lax.axis_size("sub") * blocks * VOX
    )
    grad_features, wg = local_conv(
        neighbours, block_count, me.reshape(1), grad_out, features, kmix,
        shared, scaling,
    )
    wg = butterfly_sum(wg, ("sub", "split", "brick"))
    totals = jnp.transpose(wg.reshape(channels, 27, channels), (1, 0, 2))
    return (grad_features, totals)


def solution(mesh):
    placed = (
        P(("groups", "brick", "split", "sub"), None, None),
        P(("groups", "brick", "split", "sub"), None, None),
        P(),
        P(("groups", "brick", "split", "sub")),
        P(("groups", "brick", "split", "sub"), None),
    )
    return jax.shard_map(
        on_device,
        mesh=mesh,
        in_specs=placed,
        out_specs=(P(("groups", "brick", "split", "sub"), None, None), P("groups", None, None)),
        check_vma=False,
    )
```

```python
import math

import numpy as np

import jax
import jax.numpy as jnp
from jax import lax
from jax.experimental import pallas as pl
from jax.experimental.pallas import tpu as pltpu
from jax.sharding import PartitionSpec as P

DIRECTIONS = [(a, b, c) for a in (-1, 0, 1) for b in (-1, 0, 1) for c in (-1, 0, 1)]
NEIGHBOURS = [d for d in DIRECTIONS if d != (0, 0, 0)]
VOX = 512


def from_behind(block, axis, distance):
    devices = range(lax.axis_size(axis))
    route = [((i - distance) % len(devices), i) for i in devices]
    return lax.ppermute(block, axis, route)


def butterfly_sum(x, axes):
    for axis in axes:
        n = lax.axis_size(axis)
        if n & (n - 1):
            x = lax.psum(x, axis)
            continue
        bit = 1
        while bit < n:
            x = x + lax.ppermute(x, axis, [(i, i ^ bit) for i in range(n)])
            bit *= 2
    return x


def sources_of(d):
    a, b, c = d
    found = []
    for ex in sorted({0, -a}):
        for ey in sorted({0, -b}):
            for ez in sorted({0, -c}):
                if (ex, ey, ez) != (0, 0, 0):
                    found.append((ex, ey, ez))
    return sorted(found, key=lambda e: sum(1 for t in e if t != 0))


def selectors():
    v = np.arange(VOX)
    x, y, z = v // 64, (v // 8) % 8, v % 8
    pick = np.zeros((VOX, 384), np.float32)
    place = np.zeros((256, VOX), np.float32)
    for face, (axis, side) in enumerate(((0, 0), (0, 7), (1, 0), (1, 7))):
        coord = (x, y)[axis]
        other = y if axis == 0 else x
        on = np.nonzero(coord == side)[0]
        cols = face * 64 + other[on] * 8 + z[on]
        pick[on, cols] = 1.0
        keep = on if axis == 0 else on[(x[on] != 0) & (x[on] != 7)]
        place[face * 64 + other[keep] * 8 + z[keep], keep] = 1.0
    for t, side in enumerate((0, 7)):
        on = np.nonzero(z == side)[0]
        pick[on, 256 + 64 * t + x[on] * 8 + y[on]] = 1.0
    spread = (v[None, :] // 8 == np.arange(64)[:, None]).astype(np.float32)
    as_bf16 = lambda a: jnp.asarray(a, jnp.bfloat16)
    return as_bf16(pick), as_bf16(place), as_bf16(spread)


def pack_kernel(g_ref, pick_ref, faces_ref, low_ref, high_ref):
    blocks, channels = g_ref.shape[0], g_ref.shape[1]
    g = g_ref[...].reshape(blocks * channels, VOX)
    out = jnp.dot(g, pick_ref[...], preferred_element_type=jnp.float32).astype(jnp.bfloat16)
    faces_ref[...] = out[:, 0:256].reshape(blocks, channels, 256)
    low_ref[...] = out[:, 256:320].reshape(blocks, channels, 64)
    high_ref[...] = out[:, 320:384].reshape(blocks, channels, 64)


def pack(grad_out, pick):
    blocks, channels = grad_out.shape[0], grad_out.shape[1]
    vmem = pl.BlockSpec(memory_space=pltpu.VMEM)
    return pl.pallas_call(
        pack_kernel,
        out_shape=(
            jax.ShapeDtypeStruct((blocks, channels, 256), jnp.bfloat16),
            jax.ShapeDtypeStruct((blocks, channels, 64), jnp.bfloat16),
            jax.ShapeDtypeStruct((blocks, channels, 64), jnp.bfloat16),
        ),
        in_specs=[vmem, vmem],
        out_specs=(vmem, vmem, vmem),
    )(grad_out, pick)


def make_kernel(blocks, channels, peers, scaling):
    slots = blocks * peers

    def kernel(nbr_ref, cnt_ref, me_ref, g_ref, f_ref, kmix_ref, place_ref, spread_ref, *rest):
        shared_refs = rest[:peers]
        gf_ref, wg_ref, same_ref, lay_ref, stack_ref, acc_ref = rest[peers:]
        lane = lax.broadcasted_iota(jnp.int32, (channels, VOX), 1)
        coord = (lane // 64, (lane // 8) % 8, lane % 8)

        def boundary(axis, sign):
            return coord[axis] == (7 if sign < 0 else 0)

        same_ref[slots] = jnp.zeros((channels, VOX), jnp.bfloat16)
        lay_ref[0, slots] = jnp.zeros((channels, VOX), jnp.bfloat16)
        lay_ref[1, slots] = jnp.zeros((channels, VOX), jnp.bfloat16)
        place = place_ref[...]
        spread = spread_ref[...]
        for k in range(peers):
            first = pl.ds(jnp.bitwise_xor(me_ref[0], k) * blocks, blocks)
            rows = shared_refs[k][...].reshape(blocks * channels, 384)
            wide = jnp.dot(rows[:, 0:256], place, preferred_element_type=jnp.float32)
            same_ref[first] = wide.astype(jnp.bfloat16).reshape(blocks, channels, VOX)
            for t in range(2):
                layer = rows[:, 256 + 64 * t:256 + 64 * (t + 1)]
                wide = jnp.dot(layer, spread, preferred_element_type=jnp.float32)
                lay_ref[t, first] = wide.astype(jnp.bfloat16).reshape(blocks, channels, VOX)

        gf_ref[...] = jnp.zeros_like(gf_ref)
        acc_ref[...] = jnp.zeros_like(acc_ref)

        def body(s, carry):
            own = g_ref[s]

            def neighbour(e):
                q = jnp.minimum(nbr_ref[s, NEIGHBOURS.index(e)], slots)
                if e[2] == 0:
                    return same_ref[q]
                return lay_ref[0 if e[2] < 0 else 1, q]

            for a in (-1, 0, 1):
                for b in (-1, 0, 1):
                    rx = boundary(0, -a) if a != 0 else None
                    ry = boundary(1, -b) if b != 0 else None
                    flat = own
                    if a != 0:
                        flat = jnp.where(rx, neighbour((-a, 0, 0)), flat)
                    if b != 0:
                        flat = jnp.where(ry, neighbour((0, -b, 0)), flat)
                    if a != 0 and b != 0:
                        flat = jnp.where(rx & ry, neighbour((-a, -b, 0)), flat)
                    for c in (-1, 0, 1):
                        z = flat
                        if c != 0:
                            y = neighbour((0, 0, -c))
                            if a != 0:
                                y = jnp.where(rx, neighbour((-a, 0, -c)), y)
                            if b != 0:
                                y = jnp.where(ry, neighbour((0, -b, -c)), y)
                            if a != 0 and b != 0:
                                y = jnp.where(rx & ry, neighbour((-a, -b, -c)), y)
                            z = jnp.where(boundary(2, -c), y, flat)
                        if c != 0:
                            z = jnp.where(coord[2] == (0 if c > 0 else 7),
                                          pltpu.roll(z, (-7 * c) % VOX, 1),
                                          pltpu.roll(z, c % VOX, 1))
                        if b != 0:
                            z = jnp.where(coord[1] == (0 if b > 0 else 7),
                                          pltpu.roll(z, (-56 * b) % VOX, 1),
                                          pltpu.roll(z, (8 * b) % VOX, 1))
                        if a != 0:
                            z = pltpu.roll(z, (64 * a) % VOX, 1)
                        di = 9 * (a + 1) + 3 * (b + 1) + (c + 1)
                        stack_ref[di * channels:(di + 1) * channels, :] = z
            st = stack_ref[...]
            gf = jnp.dot(kmix_ref[...], st, preferred_element_type=jnp.float32)
            gf_ref[s] = gf.astype(jnp.bfloat16)
            acc_ref[...] += lax.dot_general(
                f_ref[s], st, (((1,), (1,)), ((), ())), preferred_element_type=jnp.float32
            )
            return carry

        lax.fori_loop(0, jnp.minimum(cnt_ref[0], blocks), body, 0)
        wg_ref[...] = acc_ref[...] * scaling

    return kernel


def local_conv(neighbours, block_count, me, grad_out, features, kmix, place, spread, shared, scaling):
    blocks, channels = grad_out.shape[0], grad_out.shape[1]
    peers = len(shared)
    slots = blocks * peers
    smem = pl.BlockSpec(memory_space=pltpu.SMEM)
    vmem = pl.BlockSpec(memory_space=pltpu.VMEM)
    return pl.pallas_call(
        make_kernel(blocks, channels, peers, scaling),
        out_shape=(
            jax.ShapeDtypeStruct((blocks, channels, VOX), jnp.bfloat16),
            jax.ShapeDtypeStruct((channels, 27 * channels), jnp.float32),
        ),
        in_specs=[smem, smem, smem, vmem, vmem, vmem, vmem, vmem] + [vmem] * peers,
        out_specs=(vmem, vmem),
        scratch_shapes=[
            pltpu.VMEM((slots + 1, channels, VOX), jnp.bfloat16),
            pltpu.VMEM((2, slots + 1, channels, VOX), jnp.bfloat16),
            pltpu.VMEM((27 * channels, VOX), jnp.bfloat16),
            pltpu.VMEM((channels, 27 * channels), jnp.float32),
        ],
    )(neighbours, block_count, me, grad_out, features, kmix, place, spread, *shared)


def on_device(grad_out, features, kernel, block_count, neighbours):
    blocks, channels = grad_out.shape[0], grad_out.shape[1]
    pick, place, spread = selectors()
    faces, lowest, highest = pack(grad_out, pick)
    peers = lax.axis_size("split") * lax.axis_size("sub")
    assert peers & (peers - 1) == 0

    def spread_in_brick(x):
        return [x] + [
            lax.ppermute(x, ("split", "sub"), [(i, i ^ k) for i in range(peers)])
            for k in range(1, peers)
        ]

    from_below = from_behind(highest, "brick", 1)
    from_above = from_behind(lowest, "brick", -1)
    shared = spread_in_brick(jnp.concatenate([faces, from_below, from_above], axis=2))
    me = (lax.axis_index("split") * lax.axis_size("sub") + lax.axis_index("sub")).astype(jnp.int32)
    kmix = jnp.transpose(kernel, (1, 0, 2)).reshape(channels, 27 * channels)
    scaling = 1.0 / math.sqrt(
        lax.axis_size("brick") * lax.axis_size("split") * lax.axis_size("sub") * blocks * VOX
    )
    grad_features, wg = local_conv(
        neighbours, block_count, me.reshape(1), grad_out, features, kmix, place, spread,
        shared, scaling,
    )
    wg = butterfly_sum(wg, ("sub", "split", "brick"))
    totals = jnp.transpose(wg.reshape(channels, 27, channels), (1, 0, 2))
    return (grad_features, totals)


def solution(mesh):
    placed = (
        P(("groups", "brick", "split", "sub"), None, None),
        P(("groups", "brick", "split", "sub"), None, None),
        P(),
        P(("groups", "brick", "split", "sub")),
        P(("groups", "brick", "split", "sub"), None),
    )
    return jax.shard_map(
        on_device,
        mesh=mesh,
        in_specs=placed,
        out_specs=(P(("groups", "brick", "split", "sub"), None, None), P("groups", None, None)),
        check_vma=False,
    )
```

```python
import math

import numpy as np

import jax
import jax.numpy as jnp
from jax import lax
from jax.experimental import pallas as pl
from jax.experimental.pallas import tpu as pltpu
from jax.sharding import PartitionSpec as P

DIRECTIONS = [(a, b, c) for a in (-1, 0, 1) for b in (-1, 0, 1) for c in (-1, 0, 1)]
NEIGHBOURS = [d for d in DIRECTIONS if d != (0, 0, 0)]
VOX = 512


def from_behind(block, axis, distance):
    devices = range(lax.axis_size(axis))
    route = [((i - distance) % len(devices), i) for i in devices]
    return lax.ppermute(block, axis, route)


def butterfly_sum(x, axes, finish):
    rounds = []
    for axis in axes:
        n = lax.axis_size(axis)
        if n & (n - 1):
            rounds.append((axis, None))
            continue
        bit = 1
        while bit < n:
            rounds.append((axis, bit))
            bit *= 2
    for step, (axis, bit) in enumerate(rounds):
        last = step == len(rounds) - 1
        if bit is None:
            x = lax.psum(x, axis)
            if last:
                x = finish(x)
            continue
        other = lax.ppermute(x, axis, [(i, i ^ bit) for i in range(lax.axis_size(axis))])
        x = finish(x) + finish(other) if last else x + other
    if not rounds:
        x = finish(x)
    return x


def sources_of(d):
    a, b, c = d
    found = []
    for ex in sorted({0, -a}):
        for ey in sorted({0, -b}):
            for ez in sorted({0, -c}):
                if (ex, ey, ez) != (0, 0, 0):
                    found.append((ex, ey, ez))
    return sorted(found, key=lambda e: sum(1 for t in e if t != 0))


def selectors():
    v = np.arange(VOX)
    x, y, z = v // 64, (v // 8) % 8, v % 8
    pick = np.zeros((VOX, 384), np.float32)
    place = np.zeros((256, VOX), np.float32)
    for face, (axis, side) in enumerate(((0, 0), (0, 7), (1, 0), (1, 7))):
        coord = (x, y)[axis]
        other = y if axis == 0 else x
        on = np.nonzero(coord == side)[0]
        cols = face * 64 + other[on] * 8 + z[on]
        pick[on, cols] = 1.0
        keep = on if axis == 0 else on[(x[on] != 0) & (x[on] != 7)]
        place[face * 64 + other[keep] * 8 + z[keep], keep] = 1.0
    for t, side in enumerate((0, 7)):
        on = np.nonzero(z == side)[0]
        pick[on, 256 + 64 * t + x[on] * 8 + y[on]] = 1.0
    spread = (v[None, :] // 8 == np.arange(64)[:, None]).astype(np.float32)
    as_bf16 = lambda a: jnp.asarray(a, jnp.bfloat16)
    return as_bf16(pick), as_bf16(place), as_bf16(spread)


def pack_kernel(g_ref, pick_ref, faces_ref, low_ref, high_ref):
    blocks, channels = g_ref.shape[0], g_ref.shape[1]
    g = g_ref[...].reshape(blocks * channels, VOX)
    out = jnp.dot(g, pick_ref[...], preferred_element_type=jnp.float32).astype(jnp.bfloat16)
    faces_ref[...] = out[:, 0:256].reshape(blocks, channels, 256)
    low_ref[...] = out[:, 256:320].reshape(blocks, channels, 64)
    high_ref[...] = out[:, 320:384].reshape(blocks, channels, 64)


def pack(grad_out, pick):
    blocks, channels = grad_out.shape[0], grad_out.shape[1]
    vmem = pl.BlockSpec(memory_space=pltpu.VMEM)
    return pl.pallas_call(
        pack_kernel,
        out_shape=(
            jax.ShapeDtypeStruct((blocks, channels, 256), jnp.bfloat16),
            jax.ShapeDtypeStruct((blocks, channels, 64), jnp.bfloat16),
            jax.ShapeDtypeStruct((blocks, channels, 64), jnp.bfloat16),
        ),
        in_specs=[vmem, vmem],
        out_specs=(vmem, vmem, vmem),
    )(grad_out, pick)


def make_kernel(blocks, channels, peers, scaling):
    slots = blocks * peers

    def kernel(nbr_ref, cnt_ref, me_ref, g_ref, f_ref, kmix_ref, place_ref, spread_ref, *rest):
        face_refs = rest[:peers]
        layer_refs = rest[peers:2 * peers]
        gf_ref, wg_ref, same_ref, lay_ref, stack_ref, acc_ref = rest[2 * peers:]
        lane = lax.broadcasted_iota(jnp.int32, (channels, VOX), 1)
        coord = (lane // 64, (lane // 8) % 8, lane % 8)

        def boundary(axis, sign):
            return coord[axis] == (7 if sign < 0 else 0)

        same_ref[slots] = jnp.zeros((channels, VOX), jnp.bfloat16)
        lay_ref[0, slots] = jnp.zeros((channels, VOX), jnp.bfloat16)
        lay_ref[1, slots] = jnp.zeros((channels, VOX), jnp.bfloat16)
        place = place_ref[...]
        spread = spread_ref[...]
        for k in range(peers):
            first = pl.ds(jnp.bitwise_xor(me_ref[0], k) * blocks, blocks)
            rows = face_refs[k][...].reshape(blocks * channels, 256)
            wide = jnp.dot(rows, place, preferred_element_type=jnp.float32)
            same_ref[first] = wide.astype(jnp.bfloat16).reshape(blocks, channels, VOX)
            rows = layer_refs[k][...].reshape(blocks * channels, 128)
            for t in range(2):
                layer = rows[:, 64 * t:64 * (t + 1)]
                wide = jnp.dot(layer, spread, preferred_element_type=jnp.float32)
                lay_ref[t, first] = wide.astype(jnp.bfloat16).reshape(blocks, channels, VOX)

        gf_ref[...] = jnp.zeros_like(gf_ref)
        acc_ref[...] = jnp.zeros_like(acc_ref)

        def body(s, carry):
            own = g_ref[s]

            def neighbour(e):
                q = jnp.minimum(nbr_ref[s, NEIGHBOURS.index(e)], slots)
                if e[2] == 0:
                    return same_ref[q]
                return lay_ref[0 if e[2] < 0 else 1, q]

            for a in (-1, 0, 1):
                for b in (-1, 0, 1):
                    rx = boundary(0, -a) if a != 0 else None
                    ry = boundary(1, -b) if b != 0 else None
                    flat = own
                    if a != 0:
                        flat = jnp.where(rx, neighbour((-a, 0, 0)), flat)
                    if b != 0:
                        flat = jnp.where(ry, neighbour((0, -b, 0)), flat)
                    if a != 0 and b != 0:
                        flat = jnp.where(rx & ry, neighbour((-a, -b, 0)), flat)
                    for c in (-1, 0, 1):
                        z = flat
                        if c != 0:
                            y = neighbour((0, 0, -c))
                            if a != 0:
                                y = jnp.where(rx, neighbour((-a, 0, -c)), y)
                            if b != 0:
                                y = jnp.where(ry, neighbour((0, -b, -c)), y)
                            if a != 0 and b != 0:
                                y = jnp.where(rx & ry, neighbour((-a, -b, -c)), y)
                            z = jnp.where(boundary(2, -c), y, flat)
                        if c != 0:
                            z = jnp.where(coord[2] == (0 if c > 0 else 7),
                                          pltpu.roll(z, (-7 * c) % VOX, 1),
                                          pltpu.roll(z, c % VOX, 1))
                        if b != 0:
                            z = jnp.where(coord[1] == (0 if b > 0 else 7),
                                          pltpu.roll(z, (-56 * b) % VOX, 1),
                                          pltpu.roll(z, (8 * b) % VOX, 1))
                        if a != 0:
                            z = pltpu.roll(z, (64 * a) % VOX, 1)
                        di = 9 * (a + 1) + 3 * (b + 1) + (c + 1)
                        stack_ref[di * channels:(di + 1) * channels, :] = z
            st = stack_ref[...]
            gf = jnp.dot(kmix_ref[...], st, preferred_element_type=jnp.float32)
            gf_ref[s] = gf.astype(jnp.bfloat16)
            acc_ref[...] += lax.dot_general(
                f_ref[s], st, (((1,), (1,)), ((), ())), preferred_element_type=jnp.float32
            )
            return carry

        lax.fori_loop(0, jnp.minimum(cnt_ref[0], blocks), body, 0)
        wg_ref[...] = acc_ref[...] * scaling

    return kernel


def local_conv(neighbours, block_count, me, grad_out, features, kmix, place, spread, shared, scaling):
    blocks, channels = grad_out.shape[0], grad_out.shape[1]
    peers = len(shared) // 2
    slots = blocks * peers
    smem = pl.BlockSpec(memory_space=pltpu.SMEM)
    vmem = pl.BlockSpec(memory_space=pltpu.VMEM)
    return pl.pallas_call(
        make_kernel(blocks, channels, peers, scaling),
        out_shape=(
            jax.ShapeDtypeStruct((blocks, channels, VOX), jnp.bfloat16),
            jax.ShapeDtypeStruct((channels, 27 * channels), jnp.float32),
        ),
        in_specs=[smem, smem, smem, vmem, vmem, vmem, vmem, vmem] + [vmem] * (2 * peers),
        out_specs=(vmem, vmem),
        scratch_shapes=[
            pltpu.VMEM((slots + 1, channels, VOX), jnp.bfloat16),
            pltpu.VMEM((2, slots + 1, channels, VOX), jnp.bfloat16),
            pltpu.VMEM((27 * channels, VOX), jnp.bfloat16),
            pltpu.VMEM((channels, 27 * channels), jnp.float32),
        ],
    )(neighbours, block_count, me, grad_out, features, kmix, place, spread, *shared)


def on_device(grad_out, features, kernel, block_count, neighbours):
    blocks, channels = grad_out.shape[0], grad_out.shape[1]
    pick, place, spread = selectors()
    faces, lowest, highest = pack(grad_out, pick)
    peers = lax.axis_size("split") * lax.axis_size("sub")
    assert peers & (peers - 1) == 0

    def spread_in_brick(x):
        return [x] + [
            lax.ppermute(x, ("split", "sub"), [(i, i ^ k) for i in range(peers)])
            for k in range(1, peers)
        ]

    from_below = from_behind(highest, "brick", 1)
    from_above = from_behind(lowest, "brick", -1)
    shared = spread_in_brick(faces) + spread_in_brick(
        jnp.concatenate([from_below, from_above], axis=2)
    )
    me = (lax.axis_index("split") * lax.axis_size("sub") + lax.axis_index("sub")).astype(jnp.int32)
    kmix = jnp.transpose(kernel, (1, 0, 2)).reshape(channels, 27 * channels)
    scaling = 1.0 / math.sqrt(
        lax.axis_size("brick") * lax.axis_size("split") * lax.axis_size("sub") * blocks * VOX
    )
    grad_features, wg = local_conv(
        neighbours, block_count, me.reshape(1), grad_out, features, kmix, place, spread,
        shared, scaling,
    )
    totals = butterfly_sum(
        wg,
        ("sub", "split", "brick"),
        lambda t: jnp.transpose(t.reshape(channels, 27, channels), (1, 0, 2)),
    )
    return (grad_features, totals)


def solution(mesh):
    placed = (
        P(("groups", "brick", "split", "sub"), None, None),
        P(("groups", "brick", "split", "sub"), None, None),
        P(),
        P(("groups", "brick", "split", "sub")),
        P(("groups", "brick", "split", "sub"), None),
    )
    return jax.shard_map(
        on_device,
        mesh=mesh,
        in_specs=placed,
        out_specs=(P(("groups", "brick", "split", "sub"), None, None), P("groups", None, None)),
        check_vma=False,
    )
```

```python
import math

import numpy as np

import jax
import jax.numpy as jnp
from jax import lax
from jax.experimental import pallas as pl
from jax.experimental.pallas import tpu as pltpu
from jax.sharding import PartitionSpec as P

DIRECTIONS = [(a, b, c) for a in (-1, 0, 1) for b in (-1, 0, 1) for c in (-1, 0, 1)]
NEIGHBOURS = [d for d in DIRECTIONS if d != (0, 0, 0)]
VOX = 512


def from_behind(block, axis, distance):
    devices = range(lax.axis_size(axis))
    route = [((i - distance) % len(devices), i) for i in devices]
    return lax.ppermute(block, axis, route)


def butterfly_sum(x, axes, finish):
    rounds = []
    for axis in axes:
        n = lax.axis_size(axis)
        if n & (n - 1):
            rounds.append((axis, None))
            continue
        bit = 1
        while bit < n:
            rounds.append((axis, bit))
            bit *= 2
    for step, (axis, bit) in enumerate(rounds):
        last = step == len(rounds) - 1
        if bit is None:
            x = lax.psum(x, axis)
            if last:
                x = finish(x)
            continue
        other = lax.ppermute(x, axis, [(i, i ^ bit) for i in range(lax.axis_size(axis))])
        x = finish(x) + finish(other) if last else x + other
    if not rounds:
        x = finish(x)
    return x


def sources_of(d):
    a, b, c = d
    found = []
    for ex in sorted({0, -a}):
        for ey in sorted({0, -b}):
            for ez in sorted({0, -c}):
                if (ex, ey, ez) != (0, 0, 0):
                    found.append((ex, ey, ez))
    return sorted(found, key=lambda e: sum(1 for t in e if t != 0))


def selectors():
    v = np.arange(VOX)
    x, y, z = v // 64, (v // 8) % 8, v % 8
    pick = np.zeros((VOX, 384), np.float32)
    place = np.zeros((256, VOX), np.float32)
    for face, (axis, side) in enumerate(((0, 0), (0, 7), (1, 0), (1, 7))):
        coord = (x, y)[axis]
        other = y if axis == 0 else x
        on = np.nonzero(coord == side)[0]
        cols = face * 64 + other[on] * 8 + z[on]
        pick[on, cols] = 1.0
        keep = on if axis == 0 else on[(x[on] != 0) & (x[on] != 7)]
        place[face * 64 + other[keep] * 8 + z[keep], keep] = 1.0
    for t, side in enumerate((0, 7)):
        on = np.nonzero(z == side)[0]
        pick[on, 256 + 64 * t + x[on] * 8 + y[on]] = 1.0
    spread = (v[None, :] // 8 == np.arange(64)[:, None]).astype(np.float32)
    as_bf16 = lambda a: jnp.asarray(a, jnp.bfloat16)
    return as_bf16(pick), as_bf16(place), as_bf16(spread)


def pack_kernel(g_ref, pick_ref, faces_ref, low_ref, high_ref):
    blocks, channels = g_ref.shape[0], g_ref.shape[1]
    g = g_ref[...].reshape(blocks * channels, VOX)
    out = jnp.dot(g, pick_ref[...], preferred_element_type=jnp.float32).astype(jnp.bfloat16)
    faces_ref[...] = out[:, 0:256].reshape(blocks, channels, 256)
    low_ref[...] = out[:, 256:320].reshape(blocks, channels, 64)
    high_ref[...] = out[:, 320:384].reshape(blocks, channels, 64)


def pack(grad_out, pick):
    blocks, channels = grad_out.shape[0], grad_out.shape[1]
    vmem = pl.BlockSpec(memory_space=pltpu.VMEM)
    return pl.pallas_call(
        pack_kernel,
        out_shape=(
            jax.ShapeDtypeStruct((blocks, channels, 256), jnp.bfloat16),
            jax.ShapeDtypeStruct((blocks, channels, 64), jnp.bfloat16),
            jax.ShapeDtypeStruct((blocks, channels, 64), jnp.bfloat16),
        ),
        in_specs=[vmem, vmem],
        out_specs=(vmem, vmem, vmem),
    )(grad_out, pick)


def make_kernel(blocks, channels, peers, scaling):
    slots = blocks * peers

    def kernel(nbr_ref, cnt_ref, me_ref, g_ref, f_ref, kmix_ref, place_ref, spread_ref, *rest):
        face_refs = rest[:peers]
        layer_refs = rest[peers:2 * peers]
        gf_ref, wg_ref, same_ref, lay_ref, stack_ref, acc_ref = rest[2 * peers:]
        lane = lax.broadcasted_iota(jnp.int32, (channels, 128), 1)
        half, ycoord, zcoord = lane // 64, (lane // 8) % 8, lane % 8

        same_ref[slots] = jnp.zeros((channels, VOX), jnp.bfloat16)
        lay_ref[0, slots] = jnp.zeros((channels, VOX), jnp.bfloat16)
        lay_ref[1, slots] = jnp.zeros((channels, VOX), jnp.bfloat16)
        place = place_ref[...]
        spread = spread_ref[...]
        for k in range(peers):
            first = pl.ds(jnp.bitwise_xor(me_ref[0], k) * blocks, blocks)
            rows = face_refs[k][...].reshape(blocks * channels, 256)
            wide = jnp.dot(rows, place, preferred_element_type=jnp.float32)
            same_ref[first] = wide.astype(jnp.bfloat16).reshape(blocks, channels, VOX)
            rows = layer_refs[k][...].reshape(blocks * channels, 128)
            for t in range(2):
                layer = rows[:, 64 * t:64 * (t + 1)]
                wide = jnp.dot(layer, spread, preferred_element_type=jnp.float32)
                lay_ref[t, first] = wide.astype(jnp.bfloat16).reshape(blocks, channels, VOX)

        gf_ref[...] = jnp.zeros_like(gf_ref)
        acc_ref[...] = jnp.zeros_like(acc_ref)

        def body(s, carry):
            def own(k):
                return g_ref[s, :, 128 * k:128 * (k + 1)]

            def neighbour(e, k):
                q = jnp.minimum(nbr_ref[s, NEIGHBOURS.index(e)], slots)
                if e[2] == 0:
                    return same_ref[q, :, 128 * k:128 * (k + 1)]
                return lay_ref[0 if e[2] < 0 else 1, q, :, 128 * k:128 * (k + 1)]

            for a in (-1, 0, 1):
                kx = 3 if a > 0 else 0
                mx = half == (1 if a > 0 else 0)
                for b in (-1, 0, 1):
                    my = ycoord == (7 if b > 0 else 0)
                    flat = []
                    for k in range(4):
                        f = own(k)
                        if a != 0 and k == kx:
                            f = jnp.where(mx, neighbour((-a, 0, 0), k), f)
                        if b != 0:
                            f = jnp.where(my, neighbour((0, -b, 0), k), f)
                        if a != 0 and b != 0 and k == kx:
                            f = jnp.where(mx & my, neighbour((-a, -b, 0), k), f)
                        flat.append(f)
                    for c in (-1, 0, 1):
                        chunks = []
                        for k in range(4):
                            z = flat[k]
                            if c != 0:
                                y = neighbour((0, 0, -c), k)
                                if a != 0 and k == kx:
                                    y = jnp.where(mx, neighbour((-a, 0, -c), k), y)
                                if b != 0:
                                    y = jnp.where(my, neighbour((0, -b, -c), k), y)
                                if a != 0 and b != 0 and k == kx:
                                    y = jnp.where(mx & my, neighbour((-a, -b, -c), k), y)
                                z = jnp.where(zcoord == (0 if c > 0 else 7), y,
                                              pltpu.roll(z, c % 128, 1))
                            if b != 0:
                                z = jnp.where(ycoord == (0 if b > 0 else 7),
                                              pltpu.roll(z, (-56 * b) % 128, 1),
                                              pltpu.roll(z, (8 * b) % 128, 1))
                            chunks.append(z)
                        if a != 0:
                            turned = [pltpu.roll(z, 64, 1) for z in chunks]
                            keep = half == (1 if a > 0 else 0)
                            chunks = [jnp.where(keep, turned[k], turned[(k - a) % 4]) for k in range(4)]
                        di = 9 * (a + 1) + 3 * (b + 1) + (c + 1)
                        for k in range(4):
                            stack_ref[di * channels:(di + 1) * channels, 128 * k:128 * (k + 1)] = chunks[k]
            st = stack_ref[...]
            gf = jnp.dot(kmix_ref[...], st, preferred_element_type=jnp.float32)
            gf_ref[s] = gf.astype(jnp.bfloat16)
            acc_ref[...] += lax.dot_general(
                f_ref[s], st, (((1,), (1,)), ((), ())), preferred_element_type=jnp.float32
            )
            return carry

        lax.fori_loop(0, jnp.minimum(cnt_ref[0], blocks), body, 0)
        wg_ref[...] = acc_ref[...] * scaling

    return kernel


def local_conv(neighbours, block_count, me, grad_out, features, kmix, place, spread, shared, scaling):
    blocks, channels = grad_out.shape[0], grad_out.shape[1]
    peers = len(shared) // 2
    slots = blocks * peers
    smem = pl.BlockSpec(memory_space=pltpu.SMEM)
    vmem = pl.BlockSpec(memory_space=pltpu.VMEM)
    return pl.pallas_call(
        make_kernel(blocks, channels, peers, scaling),
        out_shape=(
            jax.ShapeDtypeStruct((blocks, channels, VOX), jnp.bfloat16),
            jax.ShapeDtypeStruct((channels, 27 * channels), jnp.float32),
        ),
        in_specs=[smem, smem, smem, vmem, vmem, vmem, vmem, vmem] + [vmem] * (2 * peers),
        out_specs=(vmem, vmem),
        scratch_shapes=[
            pltpu.VMEM((slots + 1, channels, VOX), jnp.bfloat16),
            pltpu.VMEM((2, slots + 1, channels, VOX), jnp.bfloat16),
            pltpu.VMEM((27 * channels, VOX), jnp.bfloat16),
            pltpu.VMEM((channels, 27 * channels), jnp.float32),
        ],
    )(neighbours, block_count, me, grad_out, features, kmix, place, spread, *shared)


def on_device(grad_out, features, kernel, block_count, neighbours):
    blocks, channels = grad_out.shape[0], grad_out.shape[1]
    pick, place, spread = selectors()
    faces, lowest, highest = pack(grad_out, pick)
    peers = lax.axis_size("split") * lax.axis_size("sub")
    assert peers & (peers - 1) == 0

    def spread_in_brick(x):
        return [x] + [
            lax.ppermute(x, ("split", "sub"), [(i, i ^ k) for i in range(peers)])
            for k in range(1, peers)
        ]

    from_below = from_behind(highest, "brick", 1)
    from_above = from_behind(lowest, "brick", -1)
    shared = spread_in_brick(faces) + spread_in_brick(
        jnp.concatenate([from_below, from_above], axis=2)
    )
    me = (lax.axis_index("split") * lax.axis_size("sub") + lax.axis_index("sub")).astype(jnp.int32)
    kmix = jnp.transpose(kernel, (1, 0, 2)).reshape(channels, 27 * channels)
    scaling = 1.0 / math.sqrt(
        lax.axis_size("brick") * lax.axis_size("split") * lax.axis_size("sub") * blocks * VOX
    )
    grad_features, wg = local_conv(
        neighbours, block_count, me.reshape(1), grad_out, features, kmix, place, spread,
        shared, scaling,
    )
    totals = butterfly_sum(
        wg,
        ("sub", "split", "brick"),
        lambda t: jnp.transpose(t.reshape(channels, 27, channels), (1, 0, 2)),
    )
    return (grad_features, totals)


def solution(mesh):
    placed = (
        P(("groups", "brick", "split", "sub"), None, None),
        P(("groups", "brick", "split", "sub"), None, None),
        P(),
        P(("groups", "brick", "split", "sub")),
        P(("groups", "brick", "split", "sub"), None),
    )
    return jax.shard_map(
        on_device,
        mesh=mesh,
        in_specs=placed,
        out_specs=(P(("groups", "brick", "split", "sub"), None, None), P("groups", None, None)),
        check_vma=False,
    )
```

```python
import math

import numpy as np

import jax
import jax.numpy as jnp
from jax import lax
from jax.experimental import pallas as pl
from jax.experimental.pallas import tpu as pltpu
from jax.sharding import PartitionSpec as P

DIRECTIONS = [(a, b, c) for a in (-1, 0, 1) for b in (-1, 0, 1) for c in (-1, 0, 1)]
NEIGHBOURS = [d for d in DIRECTIONS if d != (0, 0, 0)]
VOX = 512


def from_behind(block, axis, distance):
    devices = range(lax.axis_size(axis))
    route = [((i - distance) % len(devices), i) for i in devices]
    return lax.ppermute(block, axis, route)


def radix4_sum(x, axis, finish):
    n = lax.axis_size(axis)
    if n & (n - 1):
        return finish(lax.psum(x, axis))
    bits = []
    while (1 << len(bits)) < n:
        bits.append(1 << len(bits))

    def swap(v, k):
        return lax.ppermute(v, axis, [(i, i ^ k) for i in range(n)])

    while bits:
        if len(bits) >= 2:
            b0, b1 = bits[0], bits[1]
            bits = bits[2:]
            x = (x + swap(x, b0)) + (swap(x, b1) + swap(x, b0 | b1))
        else:
            x = x + swap(x, bits[0])
            bits = []
    return finish(x)


def sources_of(d):
    a, b, c = d
    found = []
    for ex in sorted({0, -a}):
        for ey in sorted({0, -b}):
            for ez in sorted({0, -c}):
                if (ex, ey, ez) != (0, 0, 0):
                    found.append((ex, ey, ez))
    return sorted(found, key=lambda e: sum(1 for t in e if t != 0))


def selectors():
    v = np.arange(VOX)
    x, y, z = v // 64, (v // 8) % 8, v % 8
    pick = np.zeros((VOX, 384), np.float32)
    place = np.zeros((256, VOX), np.float32)
    for face, (axis, side) in enumerate(((0, 0), (0, 7), (1, 0), (1, 7))):
        coord = (x, y)[axis]
        other = y if axis == 0 else x
        on = np.nonzero(coord == side)[0]
        cols = face * 64 + other[on] * 8 + z[on]
        pick[on, cols] = 1.0
        keep = on if axis == 0 else on[(x[on] != 0) & (x[on] != 7)]
        place[face * 64 + other[keep] * 8 + z[keep], keep] = 1.0
    for t, side in enumerate((0, 7)):
        on = np.nonzero(z == side)[0]
        pick[on, 256 + 64 * t + x[on] * 8 + y[on]] = 1.0
    spread = (v[None, :] // 8 == np.arange(64)[:, None]).astype(np.float32)
    as_bf16 = lambda a: jnp.asarray(a, jnp.bfloat16)
    return as_bf16(pick), as_bf16(place), as_bf16(spread)


def pack_kernel(g_ref, pick_ref, faces_ref, low_ref, high_ref):
    blocks, channels = g_ref.shape[0], g_ref.shape[1]
    g = g_ref[...].reshape(blocks * channels, VOX)
    out = jnp.dot(g, pick_ref[...], preferred_element_type=jnp.float32).astype(jnp.bfloat16)
    faces_ref[...] = out[:, 0:256].reshape(blocks, channels, 256)
    low_ref[...] = out[:, 256:320].reshape(blocks, channels, 64)
    high_ref[...] = out[:, 320:384].reshape(blocks, channels, 64)


def pack(grad_out, pick):
    blocks, channels = grad_out.shape[0], grad_out.shape[1]
    vmem = pl.BlockSpec(memory_space=pltpu.VMEM)
    return pl.pallas_call(
        pack_kernel,
        out_shape=(
            jax.ShapeDtypeStruct((blocks, channels, 256), jnp.bfloat16),
            jax.ShapeDtypeStruct((blocks, channels, 64), jnp.bfloat16),
            jax.ShapeDtypeStruct((blocks, channels, 64), jnp.bfloat16),
        ),
        in_specs=[vmem, vmem],
        out_specs=(vmem, vmem, vmem),
    )(grad_out, pick)


def make_kernel(blocks, channels, peers, scaling):
    slots = blocks * peers

    def kernel(nbr_ref, cnt_ref, me_ref, g_ref, f_ref, kmix_ref, place_ref, spread_ref, *rest):
        face_refs = rest[:peers]
        layer_refs = rest[peers:2 * peers]
        gf_ref, wg_ref, same_ref, lay_ref, stack_ref, acc_ref = rest[2 * peers:]
        lane = lax.broadcasted_iota(jnp.int32, (channels, 128), 1)
        half, ycoord, zcoord = lane // 64, (lane // 8) % 8, lane % 8

        same_ref[slots] = jnp.zeros((channels, VOX), jnp.bfloat16)
        lay_ref[0, slots] = jnp.zeros((channels, VOX), jnp.bfloat16)
        lay_ref[1, slots] = jnp.zeros((channels, VOX), jnp.bfloat16)
        place = place_ref[...]
        spread = spread_ref[...]
        for k in range(peers):
            first = pl.ds(jnp.bitwise_xor(me_ref[0], k) * blocks, blocks)
            rows = face_refs[k][...].reshape(blocks * channels, 256)
            wide = jnp.dot(rows, place, preferred_element_type=jnp.float32)
            same_ref[first] = wide.astype(jnp.bfloat16).reshape(blocks, channels, VOX)
            rows = layer_refs[k][...].reshape(blocks * channels, 128)
            for t in range(2):
                layer = rows[:, 64 * t:64 * (t + 1)]
                wide = jnp.dot(layer, spread, preferred_element_type=jnp.float32)
                lay_ref[t, first] = wide.astype(jnp.bfloat16).reshape(blocks, channels, VOX)

        gf_ref[...] = jnp.zeros_like(gf_ref)
        acc_ref[...] = jnp.zeros_like(acc_ref)

        def body(s, carry):
            def own(k):
                return g_ref[s, :, 128 * k:128 * (k + 1)]

            def neighbour(e, k):
                q = jnp.minimum(nbr_ref[s, NEIGHBOURS.index(e)], slots)
                if e[2] == 0:
                    return same_ref[q, :, 128 * k:128 * (k + 1)]
                return lay_ref[0 if e[2] < 0 else 1, q, :, 128 * k:128 * (k + 1)]

            for a in (-1, 0, 1):
                kx = 3 if a > 0 else 0
                mx = half == (1 if a > 0 else 0)
                for b in (-1, 0, 1):
                    my = ycoord == (7 if b > 0 else 0)
                    flat = []
                    for k in range(4):
                        f = own(k)
                        if a != 0 and k == kx:
                            f = jnp.where(mx, neighbour((-a, 0, 0), k), f)
                        if b != 0:
                            f = jnp.where(my, neighbour((0, -b, 0), k), f)
                        if a != 0 and b != 0 and k == kx:
                            f = jnp.where(mx & my, neighbour((-a, -b, 0), k), f)
                        flat.append(f)
                    for c in (-1, 0, 1):
                        chunks = []
                        for k in range(4):
                            z = flat[k]
                            if c != 0:
                                y = neighbour((0, 0, -c), k)
                                if a != 0 and k == kx:
                                    y = jnp.where(mx, neighbour((-a, 0, -c), k), y)
                                if b != 0:
                                    y = jnp.where(my, neighbour((0, -b, -c), k), y)
                                if a != 0 and b != 0 and k == kx:
                                    y = jnp.where(mx & my, neighbour((-a, -b, -c), k), y)
                                z = jnp.where(zcoord == (0 if c > 0 else 7), y,
                                              pltpu.roll(z, c % 128, 1))
                            if b != 0:
                                z = jnp.where(ycoord == (0 if b > 0 else 7),
                                              pltpu.roll(z, (-56 * b) % 128, 1),
                                              pltpu.roll(z, (8 * b) % 128, 1))
                            chunks.append(z)
                        if a != 0:
                            turned = [pltpu.roll(z, 64, 1) for z in chunks]
                            keep = half == (1 if a > 0 else 0)
                            chunks = [jnp.where(keep, turned[k], turned[(k - a) % 4]) for k in range(4)]
                        di = 9 * (a + 1) + 3 * (b + 1) + (c + 1)
                        for k in range(4):
                            stack_ref[di * channels:(di + 1) * channels, 128 * k:128 * (k + 1)] = chunks[k]
            st = stack_ref[...]
            gf = jnp.dot(kmix_ref[...], st, preferred_element_type=jnp.float32)
            gf_ref[s] = gf.astype(jnp.bfloat16)
            acc_ref[...] += lax.dot_general(
                f_ref[s], st, (((1,), (1,)), ((), ())), preferred_element_type=jnp.float32
            )
            return carry

        lax.fori_loop(0, jnp.minimum(cnt_ref[0], blocks), body, 0)
        wg_ref[...] = acc_ref[...] * scaling

    return kernel


def local_conv(neighbours, block_count, me, grad_out, features, kmix, place, spread, shared, scaling):
    blocks, channels = grad_out.shape[0], grad_out.shape[1]
    peers = len(shared) // 2
    slots = blocks * peers
    smem = pl.BlockSpec(memory_space=pltpu.SMEM)
    vmem = pl.BlockSpec(memory_space=pltpu.VMEM)
    return pl.pallas_call(
        make_kernel(blocks, channels, peers, scaling),
        out_shape=(
            jax.ShapeDtypeStruct((blocks, channels, VOX), jnp.bfloat16),
            jax.ShapeDtypeStruct((channels, 27 * channels), jnp.float32),
        ),
        in_specs=[smem, smem, smem, vmem, vmem, vmem, vmem, vmem] + [vmem] * (2 * peers),
        out_specs=(vmem, vmem),
        scratch_shapes=[
            pltpu.VMEM((slots + 1, channels, VOX), jnp.bfloat16),
            pltpu.VMEM((2, slots + 1, channels, VOX), jnp.bfloat16),
            pltpu.VMEM((27 * channels, VOX), jnp.bfloat16),
            pltpu.VMEM((channels, 27 * channels), jnp.float32),
        ],
    )(neighbours, block_count, me, grad_out, features, kmix, place, spread, *shared)


def on_device(grad_out, features, kernel, block_count, neighbours):
    blocks, channels = grad_out.shape[0], grad_out.shape[1]
    pick, place, spread = selectors()
    faces, lowest, highest = pack(grad_out, pick)
    peers = lax.axis_size("split") * lax.axis_size("sub")
    assert peers & (peers - 1) == 0

    def spread_in_brick(x):
        return [x] + [
            lax.ppermute(x, ("split", "sub"), [(i, i ^ k) for i in range(peers)])
            for k in range(1, peers)
        ]

    from_below = from_behind(highest, "brick", 1)
    from_above = from_behind(lowest, "brick", -1)
    shared = spread_in_brick(faces) + spread_in_brick(
        jnp.concatenate([from_below, from_above], axis=2)
    )
    me = (lax.axis_index("split") * lax.axis_size("sub") + lax.axis_index("sub")).astype(jnp.int32)
    kmix = jnp.transpose(kernel, (1, 0, 2)).reshape(channels, 27 * channels)
    scaling = 1.0 / math.sqrt(
        lax.axis_size("brick") * lax.axis_size("split") * lax.axis_size("sub") * blocks * VOX
    )
    grad_features, wg = local_conv(
        neighbours, block_count, me.reshape(1), grad_out, features, kmix, place, spread,
        shared, scaling,
    )
    wg = radix4_sum(wg, ("split", "sub"), lambda t: t)
    totals = radix4_sum(
        wg, "brick", lambda t: jnp.transpose(t.reshape(channels, 27, channels), (1, 0, 2))
    )
    return (grad_features, totals)


def solution(mesh):
    placed = (
        P(("groups", "brick", "split", "sub"), None, None),
        P(("groups", "brick", "split", "sub"), None, None),
        P(),
        P(("groups", "brick", "split", "sub")),
        P(("groups", "brick", "split", "sub"), None),
    )
    return jax.shard_map(
        on_device,
        mesh=mesh,
        in_specs=placed,
        out_specs=(P(("groups", "brick", "split", "sub"), None, None), P("groups", None, None)),
        check_vma=False,
    )
```

```python
import math

import numpy as np

import jax
import jax.numpy as jnp
from jax import lax
from jax.experimental import pallas as pl
from jax.experimental.pallas import tpu as pltpu
from jax.sharding import PartitionSpec as P

DIRECTIONS = [(a, b, c) for a in (-1, 0, 1) for b in (-1, 0, 1) for c in (-1, 0, 1)]
NEIGHBOURS = [d for d in DIRECTIONS if d != (0, 0, 0)]
VOX = 512


def from_behind(block, axis, distance):
    devices = range(lax.axis_size(axis))
    route = [((i - distance) % len(devices), i) for i in devices]
    return lax.ppermute(block, axis, route)


def butterfly_sum(x, axes, finish):
    rounds = []
    for axis in axes:
        n = lax.axis_size(axis)
        if n & (n - 1):
            rounds.append((axis, None))
            continue
        bit = 1
        while bit < n:
            rounds.append((axis, bit))
            bit *= 2
    for step, (axis, bit) in enumerate(rounds):
        last = step == len(rounds) - 1
        if bit is None:
            x = lax.psum(x, axis)
            if last:
                x = finish(x)
            continue
        other = lax.ppermute(x, axis, [(i, i ^ bit) for i in range(lax.axis_size(axis))])
        x = finish(x) + finish(other) if last else x + other
    if not rounds:
        x = finish(x)
    return x


def sources_of(d):
    a, b, c = d
    found = []
    for ex in sorted({0, -a}):
        for ey in sorted({0, -b}):
            for ez in sorted({0, -c}):
                if (ex, ey, ez) != (0, 0, 0):
                    found.append((ex, ey, ez))
    return sorted(found, key=lambda e: sum(1 for t in e if t != 0))


def selectors():
    v = np.arange(VOX)
    x, y, z = v // 64, (v // 8) % 8, v % 8
    pick = np.zeros((VOX, 384), np.float32)
    place = np.zeros((256, VOX), np.float32)
    for face, (axis, side) in enumerate(((0, 0), (0, 7), (1, 0), (1, 7))):
        coord = (x, y)[axis]
        other = y if axis == 0 else x
        on = np.nonzero(coord == side)[0]
        cols = face * 64 + other[on] * 8 + z[on]
        pick[on, cols] = 1.0
        keep = on if axis == 0 else on[(x[on] != 0) & (x[on] != 7)]
        place[face * 64 + other[keep] * 8 + z[keep], keep] = 1.0
    for t, side in enumerate((0, 7)):
        on = np.nonzero(z == side)[0]
        pick[on, 256 + 64 * t + x[on] * 8 + y[on]] = 1.0
    spread = (v[None, :] // 8 == np.arange(64)[:, None]).astype(np.float32)
    as_bf16 = lambda a: jnp.asarray(a, jnp.bfloat16)
    return as_bf16(pick), as_bf16(place), as_bf16(spread)


def pack_kernel(g_ref, pick_ref, faces_ref, low_ref, high_ref):
    blocks, channels = g_ref.shape[0], g_ref.shape[1]
    g = g_ref[...].reshape(blocks * channels, VOX)
    out = jnp.dot(g, pick_ref[...], preferred_element_type=jnp.float32).astype(jnp.bfloat16)
    faces_ref[...] = out[:, 0:256].reshape(blocks, channels, 256)
    low_ref[...] = out[:, 256:320].reshape(blocks, channels, 64)
    high_ref[...] = out[:, 320:384].reshape(blocks, channels, 64)


def pack(grad_out, pick):
    blocks, channels = grad_out.shape[0], grad_out.shape[1]
    vmem = pl.BlockSpec(memory_space=pltpu.VMEM)
    return pl.pallas_call(
        pack_kernel,
        out_shape=(
            jax.ShapeDtypeStruct((blocks, channels, 256), jnp.bfloat16),
            jax.ShapeDtypeStruct((blocks, channels, 64), jnp.bfloat16),
            jax.ShapeDtypeStruct((blocks, channels, 64), jnp.bfloat16),
        ),
        in_specs=[vmem, vmem],
        out_specs=(vmem, vmem, vmem),
    )(grad_out, pick)


def make_kernel(blocks, channels, peers, scaling):
    slots = blocks * peers

    def kernel(nbr_ref, cnt_ref, me_ref, g_ref, f_ref, kmix_ref, place_ref, spread_ref, *rest):
        face_refs = rest[:peers]
        layer_refs = rest[peers:2 * peers]
        gf_ref, wg_ref, same_ref, lay_ref, stack_ref, acc_ref = rest[2 * peers:]
        lane = lax.broadcasted_iota(jnp.int32, (channels, 128), 1)
        half, ycoord, zcoord = (
            t.astype(jnp.float32).astype(jnp.bfloat16) for t in (lane // 64, (lane // 8) % 8, lane % 8)
        )

        same_ref[slots] = jnp.zeros((channels, VOX), jnp.bfloat16)
        lay_ref[0, slots] = jnp.zeros((channels, VOX), jnp.bfloat16)
        lay_ref[1, slots] = jnp.zeros((channels, VOX), jnp.bfloat16)
        place = place_ref[...]
        spread = spread_ref[...]
        for k in range(peers):
            first = pl.ds(jnp.bitwise_xor(me_ref[0], k) * blocks, blocks)
            rows = face_refs[k][...].reshape(blocks * channels, 256)
            wide = jnp.dot(rows, place, preferred_element_type=jnp.float32)
            same_ref[first] = wide.astype(jnp.bfloat16).reshape(blocks, channels, VOX)
            rows = layer_refs[k][...].reshape(blocks * channels, 128)
            for t in range(2):
                layer = rows[:, 64 * t:64 * (t + 1)]
                wide = jnp.dot(layer, spread, preferred_element_type=jnp.float32)
                lay_ref[t, first] = wide.astype(jnp.bfloat16).reshape(blocks, channels, VOX)

        gf_ref[...] = jnp.zeros_like(gf_ref)
        acc_ref[...] = jnp.zeros_like(acc_ref)

        def body(s, carry):
            def own(k):
                return g_ref[s, :, 128 * k:128 * (k + 1)]

            def neighbour(e, k):
                q = jnp.minimum(nbr_ref[s, NEIGHBOURS.index(e)], slots)
                if e[2] == 0:
                    return same_ref[q, :, 128 * k:128 * (k + 1)]
                return lay_ref[0 if e[2] < 0 else 1, q, :, 128 * k:128 * (k + 1)]

            for a in (-1, 0, 1):
                kx = 3 if a > 0 else 0
                mx = half == (1 if a > 0 else 0)
                for b in (-1, 0, 1):
                    my = ycoord == (7 if b > 0 else 0)
                    flat = []
                    for k in range(4):
                        f = own(k)
                        if a != 0 and k == kx:
                            f = jnp.where(mx, neighbour((-a, 0, 0), k), f)
                        if b != 0:
                            f = jnp.where(my, neighbour((0, -b, 0), k), f)
                        if a != 0 and b != 0 and k == kx:
                            f = jnp.where(mx & my, neighbour((-a, -b, 0), k), f)
                        flat.append(f)
                    for c in (-1, 0, 1):
                        chunks = []
                        for k in range(4):
                            z = flat[k]
                            if c != 0:
                                y = neighbour((0, 0, -c), k)
                                if a != 0 and k == kx:
                                    y = jnp.where(mx, neighbour((-a, 0, -c), k), y)
                                if b != 0:
                                    y = jnp.where(my, neighbour((0, -b, -c), k), y)
                                if a != 0 and b != 0 and k == kx:
                                    y = jnp.where(mx & my, neighbour((-a, -b, -c), k), y)
                                z = jnp.where(zcoord == (0 if c > 0 else 7), y,
                                              pltpu.roll(z, c % 128, 1))
                            if b != 0:
                                z = jnp.where(ycoord == (0 if b > 0 else 7),
                                              pltpu.roll(z, (-56 * b) % 128, 1),
                                              pltpu.roll(z, (8 * b) % 128, 1))
                            chunks.append(z)
                        if a != 0:
                            turned = [pltpu.roll(z, 64, 1) for z in chunks]
                            keep = half == (1 if a > 0 else 0)
                            chunks = [jnp.where(keep, turned[k], turned[(k - a) % 4]) for k in range(4)]
                        di = 9 * (a + 1) + 3 * (b + 1) + (c + 1)
                        for k in range(4):
                            stack_ref[di * channels:(di + 1) * channels, 128 * k:128 * (k + 1)] = chunks[k]
            st = stack_ref[...]
            gf = jnp.dot(kmix_ref[...], st, preferred_element_type=jnp.float32)
            gf_ref[s] = gf.astype(jnp.bfloat16)
            acc_ref[...] += lax.dot_general(
                f_ref[s], st, (((1,), (1,)), ((), ())), preferred_element_type=jnp.float32
            )
            return carry

        lax.fori_loop(0, jnp.minimum(cnt_ref[0], blocks), body, 0)
        wg_ref[...] = acc_ref[...] * scaling

    return kernel


def local_conv(neighbours, block_count, me, grad_out, features, kmix, place, spread, shared, scaling):
    blocks, channels = grad_out.shape[0], grad_out.shape[1]
    peers = len(shared) // 2
    slots = blocks * peers
    smem = pl.BlockSpec(memory_space=pltpu.SMEM)
    vmem = pl.BlockSpec(memory_space=pltpu.VMEM)
    return pl.pallas_call(
        make_kernel(blocks, channels, peers, scaling),
        out_shape=(
            jax.ShapeDtypeStruct((blocks, channels, VOX), jnp.bfloat16),
            jax.ShapeDtypeStruct((channels, 27 * channels), jnp.float32),
        ),
        in_specs=[smem, smem, smem, vmem, vmem, vmem, vmem, vmem] + [vmem] * (2 * peers),
        out_specs=(vmem, vmem),
        scratch_shapes=[
            pltpu.VMEM((slots + 1, channels, VOX), jnp.bfloat16),
            pltpu.VMEM((2, slots + 1, channels, VOX), jnp.bfloat16),
            pltpu.VMEM((27 * channels, VOX), jnp.bfloat16),
            pltpu.VMEM((channels, 27 * channels), jnp.float32),
        ],
    )(neighbours, block_count, me, grad_out, features, kmix, place, spread, *shared)


def on_device(grad_out, features, kernel, block_count, neighbours):
    blocks, channels = grad_out.shape[0], grad_out.shape[1]
    pick, place, spread = selectors()
    faces, lowest, highest = pack(grad_out, pick)
    peers = lax.axis_size("split") * lax.axis_size("sub")
    assert peers & (peers - 1) == 0

    def spread_in_brick(x):
        return [x] + [
            lax.ppermute(x, ("split", "sub"), [(i, i ^ k) for i in range(peers)])
            for k in range(1, peers)
        ]

    from_below = from_behind(highest, "brick", 1)
    from_above = from_behind(lowest, "brick", -1)
    shared = spread_in_brick(faces) + spread_in_brick(
        jnp.concatenate([from_below, from_above], axis=2)
    )
    me = (lax.axis_index("split") * lax.axis_size("sub") + lax.axis_index("sub")).astype(jnp.int32)
    kmix = jnp.transpose(kernel, (1, 0, 2)).reshape(channels, 27 * channels)
    scaling = 1.0 / math.sqrt(
        lax.axis_size("brick") * lax.axis_size("split") * lax.axis_size("sub") * blocks * VOX
    )
    grad_features, wg = local_conv(
        neighbours, block_count, me.reshape(1), grad_out, features, kmix, place, spread,
        shared, scaling,
    )
    totals = butterfly_sum(
        wg,
        ("sub", "split", "brick"),
        lambda t: jnp.transpose(t.reshape(channels, 27, channels), (1, 0, 2)),
    )
    return (grad_features, totals)


def solution(mesh):
    placed = (
        P(("groups", "brick", "split", "sub"), None, None),
        P(("groups", "brick", "split", "sub"), None, None),
        P(),
        P(("groups", "brick", "split", "sub")),
        P(("groups", "brick", "split", "sub"), None),
    )
    return jax.shard_map(
        on_device,
        mesh=mesh,
        in_specs=placed,
        out_specs=(P(("groups", "brick", "split", "sub"), None, None), P("groups", None, None)),
        check_vma=False,
    )
```

```python
import math

import numpy as np

import jax
import jax.numpy as jnp
from jax import lax
from jax.experimental import pallas as pl
from jax.experimental.pallas import tpu as pltpu
from jax.sharding import PartitionSpec as P

DIRECTIONS = [(a, b, c) for a in (-1, 0, 1) for b in (-1, 0, 1) for c in (-1, 0, 1)]
NEIGHBOURS = [d for d in DIRECTIONS if d != (0, 0, 0)]
VOX = 512


def from_behind(block, axis, distance):
    devices = range(lax.axis_size(axis))
    route = [((i - distance) % len(devices), i) for i in devices]
    return lax.ppermute(block, axis, route)


def butterfly_sum(x, axes, finish):
    rounds = []
    for axis in axes:
        n = lax.axis_size(axis)
        if n & (n - 1):
            rounds.append((axis, None))
            continue
        bit = 1
        while bit < n:
            rounds.append((axis, bit))
            bit *= 2
    for step, (axis, bit) in enumerate(rounds):
        last = step == len(rounds) - 1
        if bit is None:
            x = lax.psum(x, axis)
            if last:
                x = finish(x)
            continue
        other = lax.ppermute(x, axis, [(i, i ^ bit) for i in range(lax.axis_size(axis))])
        x = finish(x) + finish(other) if last else x + other
    if not rounds:
        x = finish(x)
    return x


def sources_of(d):
    a, b, c = d
    found = []
    for ex in sorted({0, -a}):
        for ey in sorted({0, -b}):
            for ez in sorted({0, -c}):
                if (ex, ey, ez) != (0, 0, 0):
                    found.append((ex, ey, ez))
    return sorted(found, key=lambda e: sum(1 for t in e if t != 0))


def selectors():
    v = np.arange(VOX)
    x, y, z = v // 64, (v // 8) % 8, v % 8
    pick = np.zeros((VOX, 384), np.float32)
    place = np.zeros((256, VOX), np.float32)
    for face, (axis, side) in enumerate(((0, 0), (0, 7), (1, 0), (1, 7))):
        coord = (x, y)[axis]
        other = y if axis == 0 else x
        on = np.nonzero(coord == side)[0]
        cols = face * 64 + other[on] * 8 + z[on]
        pick[on, cols] = 1.0
        keep = on if axis == 0 else on[(x[on] != 0) & (x[on] != 7)]
        place[face * 64 + other[keep] * 8 + z[keep], keep] = 1.0
    for t, side in enumerate((0, 7)):
        on = np.nonzero(z == side)[0]
        pick[on, 256 + 64 * t + x[on] * 8 + y[on]] = 1.0
    spread = (v[None, :] // 8 == np.arange(64)[:, None]).astype(np.float32)
    as_bf16 = lambda a: jnp.asarray(a, jnp.bfloat16)
    return as_bf16(pick), as_bf16(place), as_bf16(spread)


def pack_kernel(g_ref, pick_ref, faces_ref, low_ref, high_ref):
    blocks, channels = g_ref.shape[0], g_ref.shape[1]
    g = g_ref[...].reshape(blocks * channels, VOX)
    out = jnp.dot(g, pick_ref[...], preferred_element_type=jnp.float32).astype(jnp.bfloat16)
    faces_ref[...] = out[:, 0:256].reshape(blocks, channels, 256)
    low_ref[...] = out[:, 256:320].reshape(blocks, channels, 64)
    high_ref[...] = out[:, 320:384].reshape(blocks, channels, 64)


def pack(grad_out, pick):
    blocks, channels = grad_out.shape[0], grad_out.shape[1]
    vmem = pl.BlockSpec(memory_space=pltpu.VMEM)
    return pl.pallas_call(
        pack_kernel,
        out_shape=(
            jax.ShapeDtypeStruct((blocks, channels, 256), jnp.bfloat16),
            jax.ShapeDtypeStruct((blocks, channels, 64), jnp.bfloat16),
            jax.ShapeDtypeStruct((blocks, channels, 64), jnp.bfloat16),
        ),
        in_specs=[vmem, vmem],
        out_specs=(vmem, vmem, vmem),
    )(grad_out, pick)


def make_kernel(blocks, channels, peers, scaling):
    slots = blocks * peers

    def kernel(nbr_ref, cnt_ref, me_ref, g_ref, f_ref, kmix_ref, place_ref, spread_ref, *rest):
        face_refs = rest[:peers]
        layer_refs = rest[peers:2 * peers]
        gf_ref, keep_ref, send_ref, same_ref, lay_ref, stack_ref, acc_ref = rest[2 * peers:]
        lane = lax.broadcasted_iota(jnp.int32, (channels, 128), 1)
        half, ycoord, zcoord = (
            t.astype(jnp.float32).astype(jnp.bfloat16) for t in (lane // 64, (lane // 8) % 8, lane % 8)
        )

        same_ref[slots] = jnp.zeros((channels, VOX), jnp.bfloat16)
        lay_ref[0, slots] = jnp.zeros((channels, VOX), jnp.bfloat16)
        lay_ref[1, slots] = jnp.zeros((channels, VOX), jnp.bfloat16)
        place = place_ref[...]
        spread = spread_ref[...]
        for k in range(peers):
            first = pl.ds(jnp.bitwise_xor(me_ref[0], k) * blocks, blocks)
            rows = face_refs[k][...].reshape(blocks * channels, 256)
            wide = jnp.dot(rows, place, preferred_element_type=jnp.float32)
            same_ref[first] = wide.astype(jnp.bfloat16).reshape(blocks, channels, VOX)
            rows = layer_refs[k][...].reshape(blocks * channels, 128)
            for t in range(2):
                layer = rows[:, 64 * t:64 * (t + 1)]
                wide = jnp.dot(layer, spread, preferred_element_type=jnp.float32)
                lay_ref[t, first] = wide.astype(jnp.bfloat16).reshape(blocks, channels, VOX)

        gf_ref[...] = jnp.zeros_like(gf_ref)
        acc_ref[...] = jnp.zeros_like(acc_ref)

        def body(s, carry):
            def own(k):
                return g_ref[s, :, 128 * k:128 * (k + 1)]

            def neighbour(e, k):
                q = jnp.minimum(nbr_ref[s, NEIGHBOURS.index(e)], slots)
                if e[2] == 0:
                    return same_ref[q, :, 128 * k:128 * (k + 1)]
                return lay_ref[0 if e[2] < 0 else 1, q, :, 128 * k:128 * (k + 1)]

            for a in (-1, 0, 1):
                kx = 3 if a > 0 else 0
                mx = half == (1 if a > 0 else 0)
                for b in (-1, 0, 1):
                    my = ycoord == (7 if b > 0 else 0)
                    flat = []
                    for k in range(4):
                        f = own(k)
                        if a != 0 and k == kx:
                            f = jnp.where(mx, neighbour((-a, 0, 0), k), f)
                        if b != 0:
                            f = jnp.where(my, neighbour((0, -b, 0), k), f)
                        if a != 0 and b != 0 and k == kx:
                            f = jnp.where(mx & my, neighbour((-a, -b, 0), k), f)
                        flat.append(f)
                    for c in (-1, 0, 1):
                        chunks = []
                        for k in range(4):
                            z = flat[k]
                            if c != 0:
                                y = neighbour((0, 0, -c), k)
                                if a != 0 and k == kx:
                                    y = jnp.where(mx, neighbour((-a, 0, -c), k), y)
                                if b != 0:
                                    y = jnp.where(my, neighbour((0, -b, -c), k), y)
                                if a != 0 and b != 0 and k == kx:
                                    y = jnp.where(mx & my, neighbour((-a, -b, -c), k), y)
                                z = jnp.where(zcoord == (0 if c > 0 else 7), y,
                                              pltpu.roll(z, c % 128, 1))
                            if b != 0:
                                z = jnp.where(ycoord == (0 if b > 0 else 7),
                                              pltpu.roll(z, (-56 * b) % 128, 1),
                                              pltpu.roll(z, (8 * b) % 128, 1))
                            chunks.append(z)
                        if a != 0:
                            turned = [pltpu.roll(z, 64, 1) for z in chunks]
                            keep = half == (1 if a > 0 else 0)
                            chunks = [jnp.where(keep, turned[k], turned[(k - a) % 4]) for k in range(4)]
                        di = 9 * (a + 1) + 3 * (b + 1) + (c + 1)
                        for k in range(4):
                            stack_ref[di * channels:(di + 1) * channels, 128 * k:128 * (k + 1)] = chunks[k]
            st = stack_ref[...]
            gf = jnp.dot(kmix_ref[...], st, preferred_element_type=jnp.float32)
            gf_ref[s] = gf.astype(jnp.bfloat16)
            acc_ref[...] += lax.dot_general(
                f_ref[s], st, (((1,), (1,)), ((), ())), preferred_element_type=jnp.float32
            )
            return carry

        lax.fori_loop(0, jnp.minimum(cnt_ref[0], blocks), body, 0)
        half_rows = channels // 2
        core = me_ref[0] % 2
        keep_ref[...] = acc_ref[pl.ds(pl.multiple_of(core * half_rows, half_rows), half_rows), :] * scaling
        send_ref[...] = (
            acc_ref[pl.ds(pl.multiple_of((1 - core) * half_rows, half_rows), half_rows), :] * scaling
        )

    return kernel


def local_conv(neighbours, block_count, me, grad_out, features, kmix, place, spread, shared, scaling):
    blocks, channels = grad_out.shape[0], grad_out.shape[1]
    peers = len(shared) // 2
    slots = blocks * peers
    smem = pl.BlockSpec(memory_space=pltpu.SMEM)
    vmem = pl.BlockSpec(memory_space=pltpu.VMEM)
    return pl.pallas_call(
        make_kernel(blocks, channels, peers, scaling),
        out_shape=(
            jax.ShapeDtypeStruct((blocks, channels, VOX), jnp.bfloat16),
            jax.ShapeDtypeStruct((channels // 2, 27 * channels), jnp.float32),
            jax.ShapeDtypeStruct((channels // 2, 27 * channels), jnp.float32),
        ),
        in_specs=[smem, smem, smem, vmem, vmem, vmem, vmem, vmem] + [vmem] * (2 * peers),
        out_specs=(vmem, vmem, vmem),
        scratch_shapes=[
            pltpu.VMEM((slots + 1, channels, VOX), jnp.bfloat16),
            pltpu.VMEM((2, slots + 1, channels, VOX), jnp.bfloat16),
            pltpu.VMEM((27 * channels, VOX), jnp.bfloat16),
            pltpu.VMEM((channels, 27 * channels), jnp.float32),
        ],
    )(neighbours, block_count, me, grad_out, features, kmix, place, spread, *shared)


def on_device(grad_out, features, kernel, block_count, neighbours):
    blocks, channels = grad_out.shape[0], grad_out.shape[1]
    pick, place, spread = selectors()
    faces, lowest, highest = pack(grad_out, pick)
    peers = lax.axis_size("split") * lax.axis_size("sub")
    assert peers & (peers - 1) == 0

    def spread_in_brick(x):
        return [x] + [
            lax.ppermute(x, ("split", "sub"), [(i, i ^ k) for i in range(peers)])
            for k in range(1, peers)
        ]

    from_below = from_behind(highest, "brick", 1)
    from_above = from_behind(lowest, "brick", -1)
    shared = spread_in_brick(faces) + spread_in_brick(
        jnp.concatenate([from_below, from_above], axis=2)
    )
    me = (lax.axis_index("split") * lax.axis_size("sub") + lax.axis_index("sub")).astype(jnp.int32)
    kmix = jnp.transpose(kernel, (1, 0, 2)).reshape(channels, 27 * channels)
    scaling = 1.0 / math.sqrt(
        lax.axis_size("brick") * lax.axis_size("split") * lax.axis_size("sub") * blocks * VOX
    )
    assert lax.axis_size("sub") == 2
    grad_features, keep, send = local_conv(
        neighbours, block_count, me.reshape(1), grad_out, features, kmix, place, spread,
        shared, scaling,
    )
    pair = [(0, 1), (1, 0)]
    half = butterfly_sum(keep + lax.ppermute(send, "sub", pair), ("split", "brick"), lambda t: t)
    other = lax.ppermute(half, "sub", pair)
    first = lax.axis_index("sub") == 0
    full = jnp.where(first, jnp.concatenate([half, other]), jnp.concatenate([other, half]))
    totals = jnp.transpose(full.reshape(channels, 27, channels), (1, 0, 2))
    return (grad_features, totals)


def solution(mesh):
    placed = (
        P(("groups", "brick", "split", "sub"), None, None),
        P(("groups", "brick", "split", "sub"), None, None),
        P(),
        P(("groups", "brick", "split", "sub")),
        P(("groups", "brick", "split", "sub"), None),
    )
    return jax.shard_map(
        on_device,
        mesh=mesh,
        in_specs=placed,
        out_specs=(P(("groups", "brick", "split", "sub"), None, None), P("groups", None, None)),
        check_vma=False,
    )
```

```python
import math

import numpy as np

import jax
import jax.numpy as jnp
from jax import lax
from jax.experimental import pallas as pl
from jax.experimental.pallas import tpu as pltpu
from jax.sharding import PartitionSpec as P

DIRECTIONS = [(a, b, c) for a in (-1, 0, 1) for b in (-1, 0, 1) for c in (-1, 0, 1)]
NEIGHBOURS = [d for d in DIRECTIONS if d != (0, 0, 0)]
VOX = 512


def from_behind(block, axis, distance):
    devices = range(lax.axis_size(axis))
    route = [((i - distance) % len(devices), i) for i in devices]
    return lax.ppermute(block, axis, route)


def butterfly_sum(x, axes, finish):
    rounds = []
    for axis in axes:
        n = lax.axis_size(axis)
        if n & (n - 1):
            rounds.append((axis, None))
            continue
        bit = 1
        while bit < n:
            rounds.append((axis, bit))
            bit *= 2
    for step, (axis, bit) in enumerate(rounds):
        last = step == len(rounds) - 1
        if bit is None:
            x = lax.psum(x, axis)
            if last:
                x = finish(x)
            continue
        other = lax.ppermute(x, axis, [(i, i ^ bit) for i in range(lax.axis_size(axis))])
        x = finish(x) + finish(other) if last else x + other
    if not rounds:
        x = finish(x)
    return x


def radix4_sum(x, axis):
    n = lax.axis_size(axis)
    if n & (n - 1):
        return lax.psum(x, axis)
    bits = []
    while (1 << len(bits)) < n:
        bits.append(1 << len(bits))

    def swap(v, k):
        return lax.ppermute(v, axis, [(i, i ^ k) for i in range(n)])

    while bits:
        if len(bits) >= 2:
            b0, b1 = bits[0], bits[1]
            bits = bits[2:]
            x = (x + swap(x, b0)) + (swap(x, b1) + swap(x, b0 | b1))
        else:
            x = x + swap(x, bits[0])
            bits = []
    return x


def sources_of(d):
    a, b, c = d
    found = []
    for ex in sorted({0, -a}):
        for ey in sorted({0, -b}):
            for ez in sorted({0, -c}):
                if (ex, ey, ez) != (0, 0, 0):
                    found.append((ex, ey, ez))
    return sorted(found, key=lambda e: sum(1 for t in e if t != 0))


def selectors():
    v = np.arange(VOX)
    x, y, z = v // 64, (v // 8) % 8, v % 8
    pick = np.zeros((VOX, 384), np.float32)
    place = np.zeros((256, VOX), np.float32)
    for face, (axis, side) in enumerate(((0, 0), (0, 7), (1, 0), (1, 7))):
        coord = (x, y)[axis]
        other = y if axis == 0 else x
        on = np.nonzero(coord == side)[0]
        cols = face * 64 + other[on] * 8 + z[on]
        pick[on, cols] = 1.0
        keep = on if axis == 0 else on[(x[on] != 0) & (x[on] != 7)]
        place[face * 64 + other[keep] * 8 + z[keep], keep] = 1.0
    for t, side in enumerate((0, 7)):
        on = np.nonzero(z == side)[0]
        pick[on, 256 + 64 * t + x[on] * 8 + y[on]] = 1.0
    spread = (v[None, :] // 8 == np.arange(64)[:, None]).astype(np.float32)
    as_bf16 = lambda a: jnp.asarray(a, jnp.bfloat16)
    return as_bf16(pick), as_bf16(place), as_bf16(spread)


def pack_kernel(g_ref, pick_ref, faces_ref, low_ref, high_ref):
    blocks, channels = g_ref.shape[0], g_ref.shape[1]
    g = g_ref[...].reshape(blocks * channels, VOX)
    out = jnp.dot(g, pick_ref[...], preferred_element_type=jnp.float32).astype(jnp.bfloat16)
    faces_ref[...] = out[:, 0:256].reshape(blocks, channels, 256)
    low_ref[...] = out[:, 256:320].reshape(blocks, channels, 64)
    high_ref[...] = out[:, 320:384].reshape(blocks, channels, 64)


def pack(grad_out, pick):
    blocks, channels = grad_out.shape[0], grad_out.shape[1]
    vmem = pl.BlockSpec(memory_space=pltpu.VMEM)
    return pl.pallas_call(
        pack_kernel,
        out_shape=(
            jax.ShapeDtypeStruct((blocks, channels, 256), jnp.bfloat16),
            jax.ShapeDtypeStruct((blocks, channels, 64), jnp.bfloat16),
            jax.ShapeDtypeStruct((blocks, channels, 64), jnp.bfloat16),
        ),
        in_specs=[vmem, vmem],
        out_specs=(vmem, vmem, vmem),
    )(grad_out, pick)


def make_kernel(blocks, channels, peers, scaling):
    slots = blocks * peers

    def kernel(nbr_ref, cnt_ref, me_ref, g_ref, f_ref, kmix_ref, place_ref, spread_ref, *rest):
        face_refs = rest[:peers]
        layer_refs = rest[peers:2 * peers]
        gf_ref, keep_ref, send_ref, same_ref, lay_ref, stack_ref, acc_ref = rest[2 * peers:]
        lane = lax.broadcasted_iota(jnp.int32, (channels, 128), 1)
        half, ycoord, zcoord = (
            t.astype(jnp.float32).astype(jnp.bfloat16) for t in (lane // 64, (lane // 8) % 8, lane % 8)
        )

        same_ref[slots] = jnp.zeros((channels, VOX), jnp.bfloat16)
        lay_ref[0, slots] = jnp.zeros((channels, VOX), jnp.bfloat16)
        lay_ref[1, slots] = jnp.zeros((channels, VOX), jnp.bfloat16)
        place = place_ref[...]
        spread = spread_ref[...]
        for k in range(peers):
            first = pl.ds(jnp.bitwise_xor(me_ref[0], k) * blocks, blocks)
            rows = face_refs[k][...].reshape(blocks * channels, 256)
            wide = jnp.dot(rows, place, preferred_element_type=jnp.float32)
            same_ref[first] = wide.astype(jnp.bfloat16).reshape(blocks, channels, VOX)
            rows = layer_refs[k][...].reshape(blocks * channels, 128)
            for t in range(2):
                layer = rows[:, 64 * t:64 * (t + 1)]
                wide = jnp.dot(layer, spread, preferred_element_type=jnp.float32)
                lay_ref[t, first] = wide.astype(jnp.bfloat16).reshape(blocks, channels, VOX)

        gf_ref[...] = jnp.zeros_like(gf_ref)
        acc_ref[...] = jnp.zeros_like(acc_ref)

        def body(s, carry):
            def own(k):
                return g_ref[s, :, 128 * k:128 * (k + 1)]

            def neighbour(e, k):
                q = jnp.minimum(nbr_ref[s, NEIGHBOURS.index(e)], slots)
                if e[2] == 0:
                    return same_ref[q, :, 128 * k:128 * (k + 1)]
                return lay_ref[0 if e[2] < 0 else 1, q, :, 128 * k:128 * (k + 1)]

            for a in (-1, 0, 1):
                kx = 3 if a > 0 else 0
                mx = half == (1 if a > 0 else 0)
                for b in (-1, 0, 1):
                    my = ycoord == (7 if b > 0 else 0)
                    flat = []
                    for k in range(4):
                        f = own(k)
                        if a != 0 and k == kx:
                            f = jnp.where(mx, neighbour((-a, 0, 0), k), f)
                        if b != 0:
                            f = jnp.where(my, neighbour((0, -b, 0), k), f)
                        if a != 0 and b != 0 and k == kx:
                            f = jnp.where(mx & my, neighbour((-a, -b, 0), k), f)
                        flat.append(f)
                    for c in (-1, 0, 1):
                        chunks = []
                        for k in range(4):
                            z = flat[k]
                            if c != 0:
                                y = neighbour((0, 0, -c), k)
                                if a != 0 and k == kx:
                                    y = jnp.where(mx, neighbour((-a, 0, -c), k), y)
                                if b != 0:
                                    y = jnp.where(my, neighbour((0, -b, -c), k), y)
                                if a != 0 and b != 0 and k == kx:
                                    y = jnp.where(mx & my, neighbour((-a, -b, -c), k), y)
                                z = jnp.where(zcoord == (0 if c > 0 else 7), y,
                                              pltpu.roll(z, c % 128, 1))
                            if b != 0:
                                z = jnp.where(ycoord == (0 if b > 0 else 7),
                                              pltpu.roll(z, (-56 * b) % 128, 1),
                                              pltpu.roll(z, (8 * b) % 128, 1))
                            chunks.append(z)
                        if a != 0:
                            turned = [pltpu.roll(z, 64, 1) for z in chunks]
                            keep = half == (1 if a > 0 else 0)
                            chunks = [jnp.where(keep, turned[k], turned[(k - a) % 4]) for k in range(4)]
                        di = 9 * (a + 1) + 3 * (b + 1) + (c + 1)
                        for k in range(4):
                            stack_ref[di * channels:(di + 1) * channels, 128 * k:128 * (k + 1)] = chunks[k]
            st = stack_ref[...]
            gf = jnp.dot(kmix_ref[...], st, preferred_element_type=jnp.float32)
            gf_ref[s] = gf.astype(jnp.bfloat16)
            acc_ref[...] += lax.dot_general(
                f_ref[s], st, (((1,), (1,)), ((), ())), preferred_element_type=jnp.float32
            )
            return carry

        lax.fori_loop(0, jnp.minimum(cnt_ref[0], blocks), body, 0)
        half_rows = channels // 2
        core = me_ref[0] % 2
        keep_ref[...] = acc_ref[pl.ds(pl.multiple_of(core * half_rows, half_rows), half_rows), :] * scaling
        send_ref[...] = (
            acc_ref[pl.ds(pl.multiple_of((1 - core) * half_rows, half_rows), half_rows), :] * scaling
        )

    return kernel


def local_conv(neighbours, block_count, me, grad_out, features, kmix, place, spread, shared, scaling):
    blocks, channels = grad_out.shape[0], grad_out.shape[1]
    peers = len(shared) // 2
    slots = blocks * peers
    smem = pl.BlockSpec(memory_space=pltpu.SMEM)
    vmem = pl.BlockSpec(memory_space=pltpu.VMEM)
    return pl.pallas_call(
        make_kernel(blocks, channels, peers, scaling),
        out_shape=(
            jax.ShapeDtypeStruct((blocks, channels, VOX), jnp.bfloat16),
            jax.ShapeDtypeStruct((channels // 2, 27 * channels), jnp.float32),
            jax.ShapeDtypeStruct((channels // 2, 27 * channels), jnp.float32),
        ),
        in_specs=[smem, smem, smem, vmem, vmem, vmem, vmem, vmem] + [vmem] * (2 * peers),
        out_specs=(vmem, vmem, vmem),
        scratch_shapes=[
            pltpu.VMEM((slots + 1, channels, VOX), jnp.bfloat16),
            pltpu.VMEM((2, slots + 1, channels, VOX), jnp.bfloat16),
            pltpu.VMEM((27 * channels, VOX), jnp.bfloat16),
            pltpu.VMEM((channels, 27 * channels), jnp.float32),
        ],
    )(neighbours, block_count, me, grad_out, features, kmix, place, spread, *shared)


def on_device(grad_out, features, kernel, block_count, neighbours):
    blocks, channels = grad_out.shape[0], grad_out.shape[1]
    pick, place, spread = selectors()
    faces, lowest, highest = pack(grad_out, pick)
    peers = lax.axis_size("split") * lax.axis_size("sub")
    assert peers & (peers - 1) == 0

    def spread_in_brick(x):
        return [x] + [
            lax.ppermute(x, ("split", "sub"), [(i, i ^ k) for i in range(peers)])
            for k in range(1, peers)
        ]

    from_below = from_behind(highest, "brick", 1)
    from_above = from_behind(lowest, "brick", -1)
    shared = spread_in_brick(faces) + spread_in_brick(
        jnp.concatenate([from_below, from_above], axis=2)
    )
    me = (lax.axis_index("split") * lax.axis_size("sub") + lax.axis_index("sub")).astype(jnp.int32)
    kmix = jnp.transpose(kernel, (1, 0, 2)).reshape(channels, 27 * channels)
    scaling = 1.0 / math.sqrt(
        lax.axis_size("brick") * lax.axis_size("split") * lax.axis_size("sub") * blocks * VOX
    )
    assert lax.axis_size("sub") == 2
    grad_features, keep, send = local_conv(
        neighbours, block_count, me.reshape(1), grad_out, features, kmix, place, spread,
        shared, scaling,
    )
    pair = [(0, 1), (1, 0)]
    half = butterfly_sum(keep + lax.ppermute(send, "sub", pair), ("split",), lambda t: t)
    half = radix4_sum(half, "brick")
    other = lax.ppermute(half, "sub", pair)
    first = lax.axis_index("sub") == 0
    full = jnp.where(first, jnp.concatenate([half, other]), jnp.concatenate([other, half]))
    totals = jnp.transpose(full.reshape(channels, 27, channels), (1, 0, 2))
    return (grad_features, totals)


def solution(mesh):
    placed = (
        P(("groups", "brick", "split", "sub"), None, None),
        P(("groups", "brick", "split", "sub"), None, None),
        P(),
        P(("groups", "brick", "split", "sub")),
        P(("groups", "brick", "split", "sub"), None),
    )
    return jax.shard_map(
        on_device,
        mesh=mesh,
        in_specs=placed,
        out_specs=(P(("groups", "brick", "split", "sub"), None, None), P("groups", None, None)),
        check_vma=False,
    )
```

```python
import math

import numpy as np

import jax
import jax.numpy as jnp
from jax import lax
from jax.experimental import pallas as pl
from jax.experimental.pallas import tpu as pltpu
from jax.sharding import PartitionSpec as P

DIRECTIONS = [(a, b, c) for a in (-1, 0, 1) for b in (-1, 0, 1) for c in (-1, 0, 1)]
NEIGHBOURS = [d for d in DIRECTIONS if d != (0, 0, 0)]
VOX = 512


def from_behind(block, axis, distance):
    devices = range(lax.axis_size(axis))
    route = [((i - distance) % len(devices), i) for i in devices]
    return lax.ppermute(block, axis, route)


def butterfly_sum(x, axes, finish):
    rounds = []
    for axis in axes:
        n = lax.axis_size(axis)
        if n & (n - 1):
            rounds.append((axis, None))
            continue
        bit = 1
        while bit < n:
            rounds.append((axis, bit))
            bit *= 2
    for step, (axis, bit) in enumerate(rounds):
        last = step == len(rounds) - 1
        if bit is None:
            x = lax.psum(x, axis)
            if last:
                x = finish(x)
            continue
        other = lax.ppermute(x, axis, [(i, i ^ bit) for i in range(lax.axis_size(axis))])
        x = finish(x) + finish(other) if last else x + other
    if not rounds:
        x = finish(x)
    return x


def radix4_sum(x, axis):
    n = lax.axis_size(axis)
    if n & (n - 1):
        return lax.psum(x, axis)
    bits = []
    while (1 << len(bits)) < n:
        bits.append(1 << len(bits))

    def swap(v, k):
        return lax.ppermute(v, axis, [(i, i ^ k) for i in range(n)])

    while bits:
        if len(bits) >= 2:
            b0, b1 = bits[0], bits[1]
            bits = bits[2:]
            x = (x + swap(x, b0)) + (swap(x, b1) + swap(x, b0 | b1))
        else:
            x = x + swap(x, bits[0])
            bits = []
    return x


def xor_group_sum(x, axes, group=3):
    n = 1
    for axis in axes:
        n *= lax.axis_size(axis)
    if n & (n - 1):
        return lax.psum(x, axes)
    nbits = n.bit_length() - 1
    for first in range(0, nbits, group):
        bits = [1 << t for t in range(first, min(first + group, nbits))]
        masks = [0]
        for b in bits:
            masks = masks + [m | b for m in masks]
        terms = {m: x if m == 0 else lax.ppermute(x, axes, [(i, i ^ m) for i in range(n)]) for m in masks}
        for b in bits:
            terms = {m: terms[m] + terms[m | b] for m in terms if not m & b}
        x = terms[0]
    return x


def sources_of(d):
    a, b, c = d
    found = []
    for ex in sorted({0, -a}):
        for ey in sorted({0, -b}):
            for ez in sorted({0, -c}):
                if (ex, ey, ez) != (0, 0, 0):
                    found.append((ex, ey, ez))
    return sorted(found, key=lambda e: sum(1 for t in e if t != 0))


def selectors():
    v = np.arange(VOX)
    x, y, z = v // 64, (v // 8) % 8, v % 8
    pick = np.zeros((VOX, 384), np.float32)
    place = np.zeros((256, VOX), np.float32)
    for face, (axis, side) in enumerate(((0, 0), (0, 7), (1, 0), (1, 7))):
        coord = (x, y)[axis]
        other = y if axis == 0 else x
        on = np.nonzero(coord == side)[0]
        cols = face * 64 + other[on] * 8 + z[on]
        pick[on, cols] = 1.0
        keep = on if axis == 0 else on[(x[on] != 0) & (x[on] != 7)]
        place[face * 64 + other[keep] * 8 + z[keep], keep] = 1.0
    for t, side in enumerate((0, 7)):
        on = np.nonzero(z == side)[0]
        pick[on, 256 + 64 * t + x[on] * 8 + y[on]] = 1.0
    spread = (v[None, :] // 8 == np.arange(64)[:, None]).astype(np.float32)
    as_bf16 = lambda a: jnp.asarray(a, jnp.bfloat16)
    return as_bf16(pick), as_bf16(place), as_bf16(spread)


def pack_kernel(g_ref, pick_ref, faces_ref, low_ref, high_ref):
    blocks, channels = g_ref.shape[0], g_ref.shape[1]
    g = g_ref[...].reshape(blocks * channels, VOX)
    out = jnp.dot(g, pick_ref[...], preferred_element_type=jnp.float32).astype(jnp.bfloat16)
    faces_ref[...] = out[:, 0:256].reshape(blocks, channels, 256)
    low_ref[...] = out[:, 256:320].reshape(blocks, channels, 64)
    high_ref[...] = out[:, 320:384].reshape(blocks, channels, 64)


def pack(grad_out, pick):
    blocks, channels = grad_out.shape[0], grad_out.shape[1]
    vmem = pl.BlockSpec(memory_space=pltpu.VMEM)
    return pl.pallas_call(
        pack_kernel,
        out_shape=(
            jax.ShapeDtypeStruct((blocks, channels, 256), jnp.bfloat16),
            jax.ShapeDtypeStruct((blocks, channels, 64), jnp.bfloat16),
            jax.ShapeDtypeStruct((blocks, channels, 64), jnp.bfloat16),
        ),
        in_specs=[vmem, vmem],
        out_specs=(vmem, vmem, vmem),
    )(grad_out, pick)


def make_kernel(blocks, channels, peers, scaling):
    slots = blocks * peers

    def kernel(nbr_ref, cnt_ref, me_ref, g_ref, f_ref, kmix_ref, place_ref, spread_ref, *rest):
        face_refs = rest[:peers]
        layer_refs = rest[peers:2 * peers]
        gf_ref, keep_ref, send_ref, same_ref, lay_ref, stack_ref, acc_ref = rest[2 * peers:]
        lane = lax.broadcasted_iota(jnp.int32, (channels, 128), 1)
        half, ycoord, zcoord = (
            t.astype(jnp.float32).astype(jnp.bfloat16) for t in (lane // 64, (lane // 8) % 8, lane % 8)
        )

        same_ref[slots] = jnp.zeros((channels, VOX), jnp.bfloat16)
        lay_ref[0, slots] = jnp.zeros((channels, VOX), jnp.bfloat16)
        lay_ref[1, slots] = jnp.zeros((channels, VOX), jnp.bfloat16)
        place = place_ref[...]
        spread = spread_ref[...]
        for k in range(peers):
            first = pl.ds(jnp.bitwise_xor(me_ref[0], k) * blocks, blocks)
            rows = face_refs[k][...].reshape(blocks * channels, 256)
            wide = jnp.dot(rows, place, preferred_element_type=jnp.float32)
            same_ref[first] = wide.astype(jnp.bfloat16).reshape(blocks, channels, VOX)
            rows = layer_refs[k][...].reshape(blocks * channels, 128)
            for t in range(2):
                layer = rows[:, 64 * t:64 * (t + 1)]
                wide = jnp.dot(layer, spread, preferred_element_type=jnp.float32)
                lay_ref[t, first] = wide.astype(jnp.bfloat16).reshape(blocks, channels, VOX)

        gf_ref[...] = jnp.zeros_like(gf_ref)
        acc_ref[...] = jnp.zeros_like(acc_ref)

        def body(s, carry):
            def own(k):
                return g_ref[s, :, 128 * k:128 * (k + 1)]

            def neighbour(e, k):
                q = jnp.minimum(nbr_ref[s, NEIGHBOURS.index(e)], slots)
                if e[2] == 0:
                    return same_ref[q, :, 128 * k:128 * (k + 1)]
                return lay_ref[0 if e[2] < 0 else 1, q, :, 128 * k:128 * (k + 1)]

            for a in (-1, 0, 1):
                kx = 3 if a > 0 else 0
                mx = half == (1 if a > 0 else 0)
                for b in (-1, 0, 1):
                    my = ycoord == (7 if b > 0 else 0)
                    flat = []
                    for k in range(4):
                        f = own(k)
                        if a != 0 and k == kx:
                            f = jnp.where(mx, neighbour((-a, 0, 0), k), f)
                        if b != 0:
                            f = jnp.where(my, neighbour((0, -b, 0), k), f)
                        if a != 0 and b != 0 and k == kx:
                            f = jnp.where(mx & my, neighbour((-a, -b, 0), k), f)
                        flat.append(f)
                    for c in (-1, 0, 1):
                        chunks = []
                        for k in range(4):
                            z = flat[k]
                            if c != 0:
                                y = neighbour((0, 0, -c), k)
                                if a != 0 and k == kx:
                                    y = jnp.where(mx, neighbour((-a, 0, -c), k), y)
                                if b != 0:
                                    y = jnp.where(my, neighbour((0, -b, -c), k), y)
                                if a != 0 and b != 0 and k == kx:
                                    y = jnp.where(mx & my, neighbour((-a, -b, -c), k), y)
                                z = jnp.where(zcoord == (0 if c > 0 else 7), y,
                                              pltpu.roll(z, c % 128, 1))
                            if b != 0:
                                z = jnp.where(ycoord == (0 if b > 0 else 7),
                                              pltpu.roll(z, (-56 * b) % 128, 1),
                                              pltpu.roll(z, (8 * b) % 128, 1))
                            chunks.append(z)
                        if a != 0:
                            turned = [pltpu.roll(z, 64, 1) for z in chunks]
                            keep = half == (1 if a > 0 else 0)
                            chunks = [jnp.where(keep, turned[k], turned[(k - a) % 4]) for k in range(4)]
                        di = 9 * (a + 1) + 3 * (b + 1) + (c + 1)
                        for k in range(4):
                            stack_ref[di * channels:(di + 1) * channels, 128 * k:128 * (k + 1)] = chunks[k]
            st = stack_ref[...]
            gf = jnp.dot(kmix_ref[...], st, preferred_element_type=jnp.float32)
            gf_ref[s] = gf.astype(jnp.bfloat16)
            acc_ref[...] += lax.dot_general(
                f_ref[s], st, (((1,), (1,)), ((), ())), preferred_element_type=jnp.float32
            )
            return carry

        lax.fori_loop(0, jnp.minimum(cnt_ref[0], blocks), body, 0)
        half_rows = channels // 2
        core = me_ref[0] % 2
        keep_ref[...] = acc_ref[pl.ds(pl.multiple_of(core * half_rows, half_rows), half_rows), :] * scaling
        send_ref[...] = (
            acc_ref[pl.ds(pl.multiple_of((1 - core) * half_rows, half_rows), half_rows), :] * scaling
        )

    return kernel


def local_conv(neighbours, block_count, me, grad_out, features, kmix, place, spread, shared, scaling):
    blocks, channels = grad_out.shape[0], grad_out.shape[1]
    peers = len(shared) // 2
    slots = blocks * peers
    smem = pl.BlockSpec(memory_space=pltpu.SMEM)
    vmem = pl.BlockSpec(memory_space=pltpu.VMEM)
    return pl.pallas_call(
        make_kernel(blocks, channels, peers, scaling),
        out_shape=(
            jax.ShapeDtypeStruct((blocks, channels, VOX), jnp.bfloat16),
            jax.ShapeDtypeStruct((channels // 2, 27 * channels), jnp.float32),
            jax.ShapeDtypeStruct((channels // 2, 27 * channels), jnp.float32),
        ),
        in_specs=[smem, smem, smem, vmem, vmem, vmem, vmem, vmem] + [vmem] * (2 * peers),
        out_specs=(vmem, vmem, vmem),
        scratch_shapes=[
            pltpu.VMEM((slots + 1, channels, VOX), jnp.bfloat16),
            pltpu.VMEM((2, slots + 1, channels, VOX), jnp.bfloat16),
            pltpu.VMEM((27 * channels, VOX), jnp.bfloat16),
            pltpu.VMEM((channels, 27 * channels), jnp.float32),
        ],
    )(neighbours, block_count, me, grad_out, features, kmix, place, spread, *shared)


def on_device(grad_out, features, kernel, block_count, neighbours):
    blocks, channels = grad_out.shape[0], grad_out.shape[1]
    pick, place, spread = selectors()
    faces, lowest, highest = pack(grad_out, pick)
    peers = lax.axis_size("split") * lax.axis_size("sub")
    assert peers & (peers - 1) == 0

    def spread_in_brick(x):
        return [x] + [
            lax.ppermute(x, ("split", "sub"), [(i, i ^ k) for i in range(peers)])
            for k in range(1, peers)
        ]

    from_below = from_behind(highest, "brick", 1)
    from_above = from_behind(lowest, "brick", -1)
    shared = spread_in_brick(faces) + spread_in_brick(
        jnp.concatenate([from_below, from_above], axis=2)
    )
    me = (lax.axis_index("split") * lax.axis_size("sub") + lax.axis_index("sub")).astype(jnp.int32)
    kmix = jnp.transpose(kernel, (1, 0, 2)).reshape(channels, 27 * channels)
    scaling = 1.0 / math.sqrt(
        lax.axis_size("brick") * lax.axis_size("split") * lax.axis_size("sub") * blocks * VOX
    )
    assert lax.axis_size("sub") == 2
    grad_features, keep, send = local_conv(
        neighbours, block_count, me.reshape(1), grad_out, features, kmix, place, spread,
        shared, scaling,
    )
    pair = [(0, 1), (1, 0)]
    half = xor_group_sum(keep + lax.ppermute(send, "sub", pair), ("brick", "split"))
    other = lax.ppermute(half, "sub", pair)
    first = lax.axis_index("sub") == 0
    full = jnp.where(first, jnp.concatenate([half, other]), jnp.concatenate([other, half]))
    totals = jnp.transpose(full.reshape(channels, 27, channels), (1, 0, 2))
    return (grad_features, totals)


def solution(mesh):
    placed = (
        P(("groups", "brick", "split", "sub"), None, None),
        P(("groups", "brick", "split", "sub"), None, None),
        P(),
        P(("groups", "brick", "split", "sub")),
        P(("groups", "brick", "split", "sub"), None),
    )
    return jax.shard_map(
        on_device,
        mesh=mesh,
        in_specs=placed,
        out_specs=(P(("groups", "brick", "split", "sub"), None, None), P("groups", None, None)),
        check_vma=False,
    )
```

```python
import math

import numpy as np

import jax
import jax.numpy as jnp
from jax import lax
from jax.experimental import pallas as pl
from jax.experimental.pallas import tpu as pltpu
from jax.sharding import PartitionSpec as P

DIRECTIONS = [(a, b, c) for a in (-1, 0, 1) for b in (-1, 0, 1) for c in (-1, 0, 1)]
NEIGHBOURS = [d for d in DIRECTIONS if d != (0, 0, 0)]
VOX = 512


def from_behind(block, axis, distance):
    devices = range(lax.axis_size(axis))
    route = [((i - distance) % len(devices), i) for i in devices]
    return lax.ppermute(block, axis, route)


def butterfly_sum(x, axes, finish):
    rounds = []
    for axis in axes:
        n = lax.axis_size(axis)
        if n & (n - 1):
            rounds.append((axis, None))
            continue
        bit = 1
        while bit < n:
            rounds.append((axis, bit))
            bit *= 2
    for step, (axis, bit) in enumerate(rounds):
        last = step == len(rounds) - 1
        if bit is None:
            x = lax.psum(x, axis)
            if last:
                x = finish(x)
            continue
        other = lax.ppermute(x, axis, [(i, i ^ bit) for i in range(lax.axis_size(axis))])
        x = finish(x) + finish(other) if last else x + other
    if not rounds:
        x = finish(x)
    return x


def radix4_sum(x, axis):
    n = lax.axis_size(axis)
    if n & (n - 1):
        return lax.psum(x, axis)
    bits = []
    while (1 << len(bits)) < n:
        bits.append(1 << len(bits))

    def swap(v, k):
        return lax.ppermute(v, axis, [(i, i ^ k) for i in range(n)])

    while bits:
        if len(bits) >= 2:
            b0, b1 = bits[0], bits[1]
            bits = bits[2:]
            x = (x + swap(x, b0)) + (swap(x, b1) + swap(x, b0 | b1))
        else:
            x = x + swap(x, bits[0])
            bits = []
    return x


def xor_group_sum(x, axes, group=3):
    n = 1
    for axis in axes:
        n *= lax.axis_size(axis)
    if n & (n - 1):
        return lax.psum(x, axes)
    nbits = n.bit_length() - 1
    for first in range(0, nbits, group):
        bits = [1 << t for t in range(first, min(first + group, nbits))]
        masks = [0]
        for b in bits:
            masks = masks + [m | b for m in masks]
        terms = {m: x if m == 0 else lax.ppermute(x, axes, [(i, i ^ m) for i in range(n)]) for m in masks}
        for b in bits:
            terms = {m: terms[m] + terms[m | b] for m in terms if not m & b}
        x = terms[0]
    return x


def sources_of(d):
    a, b, c = d
    found = []
    for ex in sorted({0, -a}):
        for ey in sorted({0, -b}):
            for ez in sorted({0, -c}):
                if (ex, ey, ez) != (0, 0, 0):
                    found.append((ex, ey, ez))
    return sorted(found, key=lambda e: sum(1 for t in e if t != 0))


def selectors():
    v = np.arange(VOX)
    x, y, z = v // 64, (v // 8) % 8, v % 8
    pick = np.zeros((VOX, 384), np.float32)
    place = np.zeros((256, VOX), np.float32)
    for face, (axis, side) in enumerate(((0, 0), (0, 7), (1, 0), (1, 7))):
        coord = (x, y)[axis]
        other = y if axis == 0 else x
        on = np.nonzero(coord == side)[0]
        cols = face * 64 + other[on] * 8 + z[on]
        pick[on, cols] = 1.0
        keep = on if axis == 0 else on[(x[on] != 0) & (x[on] != 7)]
        place[face * 64 + other[keep] * 8 + z[keep], keep] = 1.0
    for t, side in enumerate((0, 7)):
        on = np.nonzero(z == side)[0]
        pick[on, 256 + 64 * t + x[on] * 8 + y[on]] = 1.0
    spread = (v[None, :] // 8 == np.arange(64)[:, None]).astype(np.float32)
    as_bf16 = lambda a: jnp.asarray(a, jnp.bfloat16)
    return as_bf16(pick), as_bf16(place), as_bf16(spread)


def pack_kernel(g_ref, pick_ref, faces_ref, low_ref, high_ref):
    blocks, channels = g_ref.shape[0], g_ref.shape[1]
    g = g_ref[...].reshape(blocks * channels, VOX)
    out = jnp.dot(g, pick_ref[...], preferred_element_type=jnp.float32).astype(jnp.bfloat16)
    faces_ref[...] = out[:, 0:256].reshape(blocks, channels, 256)
    low_ref[...] = out[:, 256:320].reshape(blocks, channels, 64)
    high_ref[...] = out[:, 320:384].reshape(blocks, channels, 64)


def pack(grad_out, pick):
    blocks, channels = grad_out.shape[0], grad_out.shape[1]
    vmem = pl.BlockSpec(memory_space=pltpu.VMEM)
    return pl.pallas_call(
        pack_kernel,
        out_shape=(
            jax.ShapeDtypeStruct((blocks, channels, 256), jnp.bfloat16),
            jax.ShapeDtypeStruct((blocks, channels, 64), jnp.bfloat16),
            jax.ShapeDtypeStruct((blocks, channels, 64), jnp.bfloat16),
        ),
        in_specs=[vmem, vmem],
        out_specs=(vmem, vmem, vmem),
    )(grad_out, pick)


def make_kernel(blocks, channels, peers, scaling):
    slots = blocks * peers

    def kernel(nbr_ref, cnt_ref, me_ref, g_ref, f_ref, kmix_ref, place_ref, spread_ref, *rest):
        face_refs = rest[:peers]
        layer_refs = rest[peers:2 * peers]
        gf_ref, keep_ref, send_ref, same_ref, lay_ref, stack_ref, acc_ref = rest[2 * peers:]
        lane = lax.broadcasted_iota(jnp.int32, (channels, 128), 1)
        half, ycoord, zcoord = (
            t.astype(jnp.float32).astype(jnp.bfloat16) for t in (lane // 64, (lane // 8) % 8, lane % 8)
        )

        same_ref[slots] = jnp.zeros((channels, VOX), jnp.bfloat16)
        lay_ref[0, slots] = jnp.zeros((channels, VOX), jnp.bfloat16)
        lay_ref[1, slots] = jnp.zeros((channels, VOX), jnp.bfloat16)
        place = place_ref[...]
        spread = spread_ref[...]
        for k in range(peers):
            first = pl.ds(jnp.bitwise_xor(me_ref[0], k) * blocks, blocks)
            rows = face_refs[k][...].reshape(blocks * channels, 256)
            wide = jnp.dot(rows, place, preferred_element_type=jnp.float32)
            same_ref[first] = wide.astype(jnp.bfloat16).reshape(blocks, channels, VOX)
            rows = layer_refs[k][...].reshape(blocks * channels, 128)
            for t in range(2):
                layer = rows[:, 64 * t:64 * (t + 1)]
                wide = jnp.dot(layer, spread, preferred_element_type=jnp.float32)
                lay_ref[t, first] = wide.astype(jnp.bfloat16).reshape(blocks, channels, VOX)

        gf_ref[...] = jnp.zeros_like(gf_ref)
        acc_ref[...] = jnp.zeros_like(acc_ref)

        def body(s, carry):
            def own(k):
                return g_ref[s, :, 128 * k:128 * (k + 1)]

            def neighbour(e, k):
                q = jnp.minimum(nbr_ref[s, NEIGHBOURS.index(e)], slots)
                if e[2] == 0:
                    return same_ref[q, :, 128 * k:128 * (k + 1)]
                return lay_ref[0 if e[2] < 0 else 1, q, :, 128 * k:128 * (k + 1)]

            for a in (-1, 0, 1):
                kx = 3 if a > 0 else 0
                mx = half == (1 if a > 0 else 0)
                for b in (-1, 0, 1):
                    my = ycoord == (7 if b > 0 else 0)
                    flat = []
                    for k in range(4):
                        f = own(k)
                        if a != 0 and k == kx:
                            f = jnp.where(mx, neighbour((-a, 0, 0), k), f)
                        if b != 0:
                            f = jnp.where(my, neighbour((0, -b, 0), k), f)
                        if a != 0 and b != 0 and k == kx:
                            f = jnp.where(mx & my, neighbour((-a, -b, 0), k), f)
                        flat.append(f)
                    for c in (-1, 0, 1):
                        chunks = []
                        for k in range(4):
                            z = flat[k]
                            if c != 0:
                                y = neighbour((0, 0, -c), k)
                                if a != 0 and k == kx:
                                    y = jnp.where(mx, neighbour((-a, 0, -c), k), y)
                                if b != 0:
                                    y = jnp.where(my, neighbour((0, -b, -c), k), y)
                                if a != 0 and b != 0 and k == kx:
                                    y = jnp.where(mx & my, neighbour((-a, -b, -c), k), y)
                                z = jnp.where(zcoord == (0 if c > 0 else 7), y,
                                              pltpu.roll(z, c % 128, 1))
                            if b != 0:
                                z = jnp.where(ycoord == (0 if b > 0 else 7),
                                              pltpu.roll(z, (-56 * b) % 128, 1),
                                              pltpu.roll(z, (8 * b) % 128, 1))
                            chunks.append(z)
                        if a != 0:
                            turned = [pltpu.roll(z, 64, 1) for z in chunks]
                            keep = half == (1 if a > 0 else 0)
                            chunks = [jnp.where(keep, turned[k], turned[(k - a) % 4]) for k in range(4)]
                        di = 9 * (a + 1) + 3 * (b + 1) + (c + 1)
                        for k in range(4):
                            stack_ref[di * channels:(di + 1) * channels, 128 * k:128 * (k + 1)] = chunks[k]
            st = stack_ref[...]
            gf = jnp.dot(kmix_ref[...], st, preferred_element_type=jnp.float32)
            gf_ref[s] = gf.astype(jnp.bfloat16)
            acc_ref[...] += lax.dot_general(
                f_ref[s], st, (((1,), (1,)), ((), ())), preferred_element_type=jnp.float32
            )
            return carry

        lax.fori_loop(0, jnp.minimum(cnt_ref[0], blocks), body, 0)
        half_rows = channels // 2
        core = me_ref[0] % 2
        keep_ref[...] = acc_ref[pl.ds(pl.multiple_of(core * half_rows, half_rows), half_rows), :] * scaling
        send_ref[...] = (
            acc_ref[pl.ds(pl.multiple_of((1 - core) * half_rows, half_rows), half_rows), :] * scaling
        )

    return kernel


def local_conv(neighbours, block_count, me, grad_out, features, kmix, place, spread, shared, scaling):
    blocks, channels = grad_out.shape[0], grad_out.shape[1]
    peers = len(shared) // 2
    slots = blocks * peers
    smem = pl.BlockSpec(memory_space=pltpu.SMEM)
    vmem = pl.BlockSpec(memory_space=pltpu.VMEM)
    return pl.pallas_call(
        make_kernel(blocks, channels, peers, scaling),
        out_shape=(
            jax.ShapeDtypeStruct((blocks, channels, VOX), jnp.bfloat16),
            jax.ShapeDtypeStruct((channels // 2, 27 * channels), jnp.float32),
            jax.ShapeDtypeStruct((channels // 2, 27 * channels), jnp.float32),
        ),
        in_specs=[smem, smem, smem, vmem, vmem, vmem, vmem, vmem] + [vmem] * (2 * peers),
        out_specs=(vmem, vmem, vmem),
        scratch_shapes=[
            pltpu.VMEM((slots + 1, channels, VOX), jnp.bfloat16),
            pltpu.VMEM((2, slots + 1, channels, VOX), jnp.bfloat16),
            pltpu.VMEM((27 * channels, VOX), jnp.bfloat16),
            pltpu.VMEM((channels, 27 * channels), jnp.float32),
        ],
    )(neighbours, block_count, me, grad_out, features, kmix, place, spread, *shared)


def on_device(grad_out, features, kernel, block_count, neighbours):
    blocks, channels = grad_out.shape[0], grad_out.shape[1]
    pick, place, spread = selectors()
    faces, lowest, highest = pack(grad_out, pick)
    peers = lax.axis_size("split") * lax.axis_size("sub")
    assert peers & (peers - 1) == 0

    def spread_in_brick(x):
        return [x] + [
            lax.ppermute(x, ("split", "sub"), [(i, i ^ k) for i in range(peers)])
            for k in range(1, peers)
        ]

    from_below = from_behind(highest, "brick", 1)
    from_above = from_behind(lowest, "brick", -1)
    shared = spread_in_brick(faces) + spread_in_brick(
        jnp.concatenate([from_below, from_above], axis=2)
    )
    me = (lax.axis_index("split") * lax.axis_size("sub") + lax.axis_index("sub")).astype(jnp.int32)
    kmix = jnp.transpose(kernel, (1, 0, 2)).reshape(channels, 27 * channels)
    scaling = 1.0 / math.sqrt(
        lax.axis_size("brick") * lax.axis_size("split") * lax.axis_size("sub") * blocks * VOX
    )
    assert lax.axis_size("sub") == 2
    grad_features, keep, send = local_conv(
        neighbours, block_count, me.reshape(1), grad_out, features, kmix, place, spread,
        shared, scaling,
    )
    pair = [(0, 1), (1, 0)]
    half = xor_group_sum(keep + lax.ppermute(send, "sub", pair), ("brick", "split"), group=2)
    other = lax.ppermute(half, "sub", pair)
    first = lax.axis_index("sub") == 0
    full = jnp.where(first, jnp.concatenate([half, other]), jnp.concatenate([other, half]))
    totals = jnp.transpose(full.reshape(channels, 27, channels), (1, 0, 2))
    return (grad_features, totals)


def solution(mesh):
    placed = (
        P(("groups", "brick", "split", "sub"), None, None),
        P(("groups", "brick", "split", "sub"), None, None),
        P(),
        P(("groups", "brick", "split", "sub")),
        P(("groups", "brick", "split", "sub"), None),
    )
    return jax.shard_map(
        on_device,
        mesh=mesh,
        in_specs=placed,
        out_specs=(P(("groups", "brick", "split", "sub"), None, None), P("groups", None, None)),
        check_vma=False,
    )
```

```python
import math

import numpy as np

import jax
import jax.numpy as jnp
from jax import lax
from jax.experimental import pallas as pl
from jax.experimental.pallas import tpu as pltpu
from jax.sharding import PartitionSpec as P

DIRECTIONS = [(a, b, c) for a in (-1, 0, 1) for b in (-1, 0, 1) for c in (-1, 0, 1)]
NEIGHBOURS = [d for d in DIRECTIONS if d != (0, 0, 0)]
VOX = 512


def from_behind(block, axis, distance):
    devices = range(lax.axis_size(axis))
    route = [((i - distance) % len(devices), i) for i in devices]
    return lax.ppermute(block, axis, route)


def butterfly_sum(x, axes, finish):
    rounds = []
    for axis in axes:
        n = lax.axis_size(axis)
        if n & (n - 1):
            rounds.append((axis, None))
            continue
        bit = 1
        while bit < n:
            rounds.append((axis, bit))
            bit *= 2
    for step, (axis, bit) in enumerate(rounds):
        last = step == len(rounds) - 1
        if bit is None:
            x = lax.psum(x, axis)
            if last:
                x = finish(x)
            continue
        other = lax.ppermute(x, axis, [(i, i ^ bit) for i in range(lax.axis_size(axis))])
        x = finish(x) + finish(other) if last else x + other
    if not rounds:
        x = finish(x)
    return x


def radix4_sum(x, axis):
    n = lax.axis_size(axis)
    if n & (n - 1):
        return lax.psum(x, axis)
    bits = []
    while (1 << len(bits)) < n:
        bits.append(1 << len(bits))

    def swap(v, k):
        return lax.ppermute(v, axis, [(i, i ^ k) for i in range(n)])

    while bits:
        if len(bits) >= 2:
            b0, b1 = bits[0], bits[1]
            bits = bits[2:]
            x = (x + swap(x, b0)) + (swap(x, b1) + swap(x, b0 | b1))
        else:
            x = x + swap(x, bits[0])
            bits = []
    return x


def xor_group_sum(x, axes, group=3):
    n = 1
    for axis in axes:
        n *= lax.axis_size(axis)
    if n & (n - 1):
        return lax.psum(x, axes)
    nbits = n.bit_length() - 1
    for first in range(0, nbits, group):
        bits = [1 << t for t in range(first, min(first + group, nbits))]
        masks = [0]
        for b in bits:
            masks = masks + [m | b for m in masks]
        terms = {m: x if m == 0 else lax.ppermute(x, axes, [(i, i ^ m) for i in range(n)]) for m in masks}
        for b in bits:
            terms = {m: terms[m] + terms[m | b] for m in terms if not m & b}
        x = terms[0]
    return x


def sources_of(d):
    a, b, c = d
    found = []
    for ex in sorted({0, -a}):
        for ey in sorted({0, -b}):
            for ez in sorted({0, -c}):
                if (ex, ey, ez) != (0, 0, 0):
                    found.append((ex, ey, ez))
    return sorted(found, key=lambda e: sum(1 for t in e if t != 0))


def selectors():
    v = np.arange(VOX)
    x, y, z = v // 64, (v // 8) % 8, v % 8
    pick = np.zeros((VOX, 384), np.float32)
    place = np.zeros((256, VOX), np.float32)
    for face, (axis, side) in enumerate(((0, 0), (0, 7), (1, 0), (1, 7))):
        coord = (x, y)[axis]
        other = y if axis == 0 else x
        on = np.nonzero(coord == side)[0]
        cols = face * 64 + other[on] * 8 + z[on]
        pick[on, cols] = 1.0
        keep = on if axis == 0 else on[(x[on] != 0) & (x[on] != 7)]
        place[face * 64 + other[keep] * 8 + z[keep], keep] = 1.0
    for t, side in enumerate((0, 7)):
        on = np.nonzero(z == side)[0]
        pick[on, 256 + 64 * t + x[on] * 8 + y[on]] = 1.0
    spread = (v[None, :] // 8 == np.arange(64)[:, None]).astype(np.float32)
    as_bf16 = lambda a: jnp.asarray(a, jnp.bfloat16)
    return as_bf16(pick[:, 128:]), as_bf16(place), as_bf16(spread)


def pack_kernel(g_ref, pick_ref, faces_ref, low_ref, high_ref):
    blocks, channels = g_ref.shape[0], g_ref.shape[1]
    g = g_ref[...].reshape(blocks * channels, VOX)
    out = jnp.dot(g, pick_ref[...], preferred_element_type=jnp.float32).astype(jnp.bfloat16)
    lane = lax.broadcasted_iota(jnp.int32, (blocks * channels, 128), 1)
    x_faces = jnp.where(lane < 64, g[:, 0:128], g[:, 384:512])
    faces_ref[...] = jnp.concatenate([x_faces, out[:, 0:128]], axis=1).reshape(blocks, channels, 256)
    low_ref[...] = out[:, 128:192].reshape(blocks, channels, 64)
    high_ref[...] = out[:, 192:256].reshape(blocks, channels, 64)


def pack(grad_out, pick):
    blocks, channels = grad_out.shape[0], grad_out.shape[1]
    vmem = pl.BlockSpec(memory_space=pltpu.VMEM)
    return pl.pallas_call(
        pack_kernel,
        out_shape=(
            jax.ShapeDtypeStruct((blocks, channels, 256), jnp.bfloat16),
            jax.ShapeDtypeStruct((blocks, channels, 64), jnp.bfloat16),
            jax.ShapeDtypeStruct((blocks, channels, 64), jnp.bfloat16),
        ),
        in_specs=[vmem, vmem],
        out_specs=(vmem, vmem, vmem),
    )(grad_out, pick)


def make_kernel(blocks, channels, peers, scaling):
    slots = blocks * peers

    def kernel(nbr_ref, cnt_ref, me_ref, g_ref, f_ref, kmix_ref, place_ref, spread_ref, *rest):
        face_refs = rest[:peers]
        layer_refs = rest[peers:2 * peers]
        gf_ref, keep_ref, send_ref, same_ref, lay_ref, stack_ref, acc_ref = rest[2 * peers:]
        lane = lax.broadcasted_iota(jnp.int32, (channels, 128), 1)
        half, ycoord, zcoord = (
            t.astype(jnp.float32).astype(jnp.bfloat16) for t in (lane // 64, (lane // 8) % 8, lane % 8)
        )

        same_ref[slots] = jnp.zeros((channels, VOX), jnp.bfloat16)
        lay_ref[0, slots] = jnp.zeros((channels, VOX), jnp.bfloat16)
        lay_ref[1, slots] = jnp.zeros((channels, VOX), jnp.bfloat16)
        place = place_ref[...]
        spread = spread_ref[...]
        for k in range(peers):
            first = pl.ds(jnp.bitwise_xor(me_ref[0], k) * blocks, blocks)
            rows = face_refs[k][...].reshape(blocks * channels, 256)
            wide = jnp.dot(rows, place, preferred_element_type=jnp.float32)
            same_ref[first] = wide.astype(jnp.bfloat16).reshape(blocks, channels, VOX)
            rows = layer_refs[k][...].reshape(blocks * channels, 128)
            for t in range(2):
                layer = rows[:, 64 * t:64 * (t + 1)]
                wide = jnp.dot(layer, spread, preferred_element_type=jnp.float32)
                lay_ref[t, first] = wide.astype(jnp.bfloat16).reshape(blocks, channels, VOX)

        gf_ref[...] = jnp.zeros_like(gf_ref)
        acc_ref[...] = jnp.zeros_like(acc_ref)

        def body(s, carry):
            def own(k):
                return g_ref[s, :, 128 * k:128 * (k + 1)]

            def neighbour(e, k):
                q = jnp.minimum(nbr_ref[s, NEIGHBOURS.index(e)], slots)
                if e[2] == 0:
                    return same_ref[q, :, 128 * k:128 * (k + 1)]
                return lay_ref[0 if e[2] < 0 else 1, q, :, 128 * k:128 * (k + 1)]

            for a in (-1, 0, 1):
                kx = 3 if a > 0 else 0
                mx = half == (1 if a > 0 else 0)
                for b in (-1, 0, 1):
                    my = ycoord == (7 if b > 0 else 0)
                    flat = []
                    for k in range(4):
                        f = own(k)
                        if a != 0 and k == kx:
                            f = jnp.where(mx, neighbour((-a, 0, 0), k), f)
                        if b != 0:
                            f = jnp.where(my, neighbour((0, -b, 0), k), f)
                        if a != 0 and b != 0 and k == kx:
                            f = jnp.where(mx & my, neighbour((-a, -b, 0), k), f)
                        flat.append(f)
                    for c in (-1, 0, 1):
                        chunks = []
                        for k in range(4):
                            z = flat[k]
                            if c != 0:
                                y = neighbour((0, 0, -c), k)
                                if a != 0 and k == kx:
                                    y = jnp.where(mx, neighbour((-a, 0, -c), k), y)
                                if b != 0:
                                    y = jnp.where(my, neighbour((0, -b, -c), k), y)
                                if a != 0 and b != 0 and k == kx:
                                    y = jnp.where(mx & my, neighbour((-a, -b, -c), k), y)
                                z = jnp.where(zcoord == (0 if c > 0 else 7), y,
                                              pltpu.roll(z, c % 128, 1))
                            if b != 0:
                                z = jnp.where(ycoord == (0 if b > 0 else 7),
                                              pltpu.roll(z, (-56 * b) % 128, 1),
                                              pltpu.roll(z, (8 * b) % 128, 1))
                            chunks.append(z)
                        if a != 0:
                            turned = [pltpu.roll(z, 64, 1) for z in chunks]
                            keep = half == (1 if a > 0 else 0)
                            chunks = [jnp.where(keep, turned[k], turned[(k - a) % 4]) for k in range(4)]
                        di = 9 * (a + 1) + 3 * (b + 1) + (c + 1)
                        for k in range(4):
                            stack_ref[di * channels:(di + 1) * channels, 128 * k:128 * (k + 1)] = chunks[k]
            st = stack_ref[...]
            gf = jnp.dot(kmix_ref[...], st, preferred_element_type=jnp.float32)
            gf_ref[s] = gf.astype(jnp.bfloat16)
            acc_ref[...] += lax.dot_general(
                f_ref[s], st, (((1,), (1,)), ((), ())), preferred_element_type=jnp.float32
            )
            return carry

        lax.fori_loop(0, jnp.minimum(cnt_ref[0], blocks), body, 0)
        half_rows = channels // 2
        core = me_ref[0] % 2
        keep_ref[...] = acc_ref[pl.ds(pl.multiple_of(core * half_rows, half_rows), half_rows), :] * scaling
        send_ref[...] = (
            acc_ref[pl.ds(pl.multiple_of((1 - core) * half_rows, half_rows), half_rows), :] * scaling
        )

    return kernel


def local_conv(neighbours, block_count, me, grad_out, features, kmix, place, spread, shared, scaling):
    blocks, channels = grad_out.shape[0], grad_out.shape[1]
    peers = len(shared) // 2
    slots = blocks * peers
    smem = pl.BlockSpec(memory_space=pltpu.SMEM)
    vmem = pl.BlockSpec(memory_space=pltpu.VMEM)
    return pl.pallas_call(
        make_kernel(blocks, channels, peers, scaling),
        out_shape=(
            jax.ShapeDtypeStruct((blocks, channels, VOX), jnp.bfloat16),
            jax.ShapeDtypeStruct((channels // 2, 27 * channels), jnp.float32),
            jax.ShapeDtypeStruct((channels // 2, 27 * channels), jnp.float32),
        ),
        in_specs=[smem, smem, smem, vmem, vmem, vmem, vmem, vmem] + [vmem] * (2 * peers),
        out_specs=(vmem, vmem, vmem),
        scratch_shapes=[
            pltpu.VMEM((slots + 1, channels, VOX), jnp.bfloat16),
            pltpu.VMEM((2, slots + 1, channels, VOX), jnp.bfloat16),
            pltpu.VMEM((27 * channels, VOX), jnp.bfloat16),
            pltpu.VMEM((channels, 27 * channels), jnp.float32),
        ],
    )(neighbours, block_count, me, grad_out, features, kmix, place, spread, *shared)


def on_device(grad_out, features, kernel, block_count, neighbours):
    blocks, channels = grad_out.shape[0], grad_out.shape[1]
    pick, place, spread = selectors()
    faces, lowest, highest = pack(grad_out, pick)
    peers = lax.axis_size("split") * lax.axis_size("sub")
    assert peers & (peers - 1) == 0

    def spread_in_brick(x):
        return [x] + [
            lax.ppermute(x, ("split", "sub"), [(i, i ^ k) for i in range(peers)])
            for k in range(1, peers)
        ]

    from_below = from_behind(highest, "brick", 1)
    from_above = from_behind(lowest, "brick", -1)
    shared = spread_in_brick(faces) + spread_in_brick(
        jnp.concatenate([from_below, from_above], axis=2)
    )
    me = (lax.axis_index("split") * lax.axis_size("sub") + lax.axis_index("sub")).astype(jnp.int32)
    kmix = jnp.transpose(kernel, (1, 0, 2)).reshape(channels, 27 * channels)
    scaling = 1.0 / math.sqrt(
        lax.axis_size("brick") * lax.axis_size("split") * lax.axis_size("sub") * blocks * VOX
    )
    assert lax.axis_size("sub") == 2
    grad_features, keep, send = local_conv(
        neighbours, block_count, me.reshape(1), grad_out, features, kmix, place, spread,
        shared, scaling,
    )
    pair = [(0, 1), (1, 0)]
    half = xor_group_sum(keep + lax.ppermute(send, "sub", pair), ("brick", "split"), group=2)
    other = lax.ppermute(half, "sub", pair)
    first = lax.axis_index("sub") == 0
    full = jnp.where(first, jnp.concatenate([half, other]), jnp.concatenate([other, half]))
    totals = jnp.transpose(full.reshape(channels, 27, channels), (1, 0, 2))
    return (grad_features, totals)


def solution(mesh):
    placed = (
        P(("groups", "brick", "split", "sub"), None, None),
        P(("groups", "brick", "split", "sub"), None, None),
        P(),
        P(("groups", "brick", "split", "sub")),
        P(("groups", "brick", "split", "sub"), None),
    )
    return jax.shard_map(
        on_device,
        mesh=mesh,
        in_specs=placed,
        out_specs=(P(("groups", "brick", "split", "sub"), None, None), P("groups", None, None)),
        check_vma=False,
    )
```

```python
import math

import numpy as np

import jax
import jax.numpy as jnp
from jax import lax
from jax.experimental import pallas as pl
from jax.experimental.pallas import tpu as pltpu
from jax.sharding import PartitionSpec as P

DIRECTIONS = [(a, b, c) for a in (-1, 0, 1) for b in (-1, 0, 1) for c in (-1, 0, 1)]
NEIGHBOURS = [d for d in DIRECTIONS if d != (0, 0, 0)]
VOX = 512


def from_behind(block, axis, distance):
    devices = range(lax.axis_size(axis))
    route = [((i - distance) % len(devices), i) for i in devices]
    return lax.ppermute(block, axis, route)


def butterfly_sum(x, axes, finish):
    rounds = []
    for axis in axes:
        n = lax.axis_size(axis)
        if n & (n - 1):
            rounds.append((axis, None))
            continue
        bit = 1
        while bit < n:
            rounds.append((axis, bit))
            bit *= 2
    for step, (axis, bit) in enumerate(rounds):
        last = step == len(rounds) - 1
        if bit is None:
            x = lax.psum(x, axis)
            if last:
                x = finish(x)
            continue
        other = lax.ppermute(x, axis, [(i, i ^ bit) for i in range(lax.axis_size(axis))])
        x = finish(x) + finish(other) if last else x + other
    if not rounds:
        x = finish(x)
    return x


def radix4_sum(x, axis):
    n = lax.axis_size(axis)
    if n & (n - 1):
        return lax.psum(x, axis)
    bits = []
    while (1 << len(bits)) < n:
        bits.append(1 << len(bits))

    def swap(v, k):
        return lax.ppermute(v, axis, [(i, i ^ k) for i in range(n)])

    while bits:
        if len(bits) >= 2:
            b0, b1 = bits[0], bits[1]
            bits = bits[2:]
            x = (x + swap(x, b0)) + (swap(x, b1) + swap(x, b0 | b1))
        else:
            x = x + swap(x, bits[0])
            bits = []
    return x


def xor_group_sum(x, axes, group=3):
    n = 1
    for axis in axes:
        n *= lax.axis_size(axis)
    if n & (n - 1):
        return lax.psum(x, axes)
    nbits = n.bit_length() - 1
    starts = list(range(0, nbits, group))
    for first in reversed(starts):
        bits = [1 << t for t in range(first, min(first + group, nbits))]
        masks = [0]
        for b in bits:
            masks = masks + [m | b for m in masks]
        terms = {m: x if m == 0 else lax.ppermute(x, axes, [(i, i ^ m) for i in range(n)]) for m in masks}
        for b in bits:
            terms = {m: terms[m] + terms[m | b] for m in terms if not m & b}
        x = terms[0]
    return x


def sources_of(d):
    a, b, c = d
    found = []
    for ex in sorted({0, -a}):
        for ey in sorted({0, -b}):
            for ez in sorted({0, -c}):
                if (ex, ey, ez) != (0, 0, 0):
                    found.append((ex, ey, ez))
    return sorted(found, key=lambda e: sum(1 for t in e if t != 0))


def selectors():
    v = np.arange(VOX)
    x, y, z = v // 64, (v // 8) % 8, v % 8
    pick = np.zeros((VOX, 384), np.float32)
    place = np.zeros((256, VOX), np.float32)
    for face, (axis, side) in enumerate(((0, 0), (0, 7), (1, 0), (1, 7))):
        coord = (x, y)[axis]
        other = y if axis == 0 else x
        on = np.nonzero(coord == side)[0]
        cols = face * 64 + other[on] * 8 + z[on]
        pick[on, cols] = 1.0
        keep = on if axis == 0 else on[(x[on] != 0) & (x[on] != 7)]
        place[face * 64 + other[keep] * 8 + z[keep], keep] = 1.0
    for t, side in enumerate((0, 7)):
        on = np.nonzero(z == side)[0]
        pick[on, 256 + 64 * t + x[on] * 8 + y[on]] = 1.0
    spread = (v[None, :] // 8 == np.arange(64)[:, None]).astype(np.float32)
    as_bf16 = lambda a: jnp.asarray(a, jnp.bfloat16)
    return as_bf16(pick), as_bf16(place), as_bf16(spread)


def pack_kernel(g_ref, pick_ref, faces_ref, low_ref, high_ref):
    blocks, channels = g_ref.shape[0], g_ref.shape[1]
    g = g_ref[...].reshape(blocks * channels, VOX)
    out = jnp.dot(g, pick_ref[...], preferred_element_type=jnp.float32).astype(jnp.bfloat16)
    faces_ref[...] = out[:, 0:256].reshape(blocks, channels, 256)
    low_ref[...] = out[:, 256:320].reshape(blocks, channels, 64)
    high_ref[...] = out[:, 320:384].reshape(blocks, channels, 64)


def pack(grad_out, pick):
    blocks, channels = grad_out.shape[0], grad_out.shape[1]
    vmem = pl.BlockSpec(memory_space=pltpu.VMEM)
    return pl.pallas_call(
        pack_kernel,
        out_shape=(
            jax.ShapeDtypeStruct((blocks, channels, 256), jnp.bfloat16),
            jax.ShapeDtypeStruct((blocks, channels, 64), jnp.bfloat16),
            jax.ShapeDtypeStruct((blocks, channels, 64), jnp.bfloat16),
        ),
        in_specs=[vmem, vmem],
        out_specs=(vmem, vmem, vmem),
    )(grad_out, pick)


def make_kernel(blocks, channels, peers, scaling):
    slots = blocks * peers

    def kernel(nbr_ref, cnt_ref, me_ref, g_ref, f_ref, kmix_ref, place_ref, spread_ref, *rest):
        face_refs = rest[:peers]
        layer_refs = rest[peers:2 * peers]
        gf_ref, keep_ref, send_ref, same_ref, lay_ref, stack_ref, acc_ref = rest[2 * peers:]
        lane = lax.broadcasted_iota(jnp.int32, (channels, 128), 1)
        half, ycoord, zcoord = (
            t.astype(jnp.float32).astype(jnp.bfloat16) for t in (lane // 64, (lane // 8) % 8, lane % 8)
        )

        same_ref[slots] = jnp.zeros((channels, VOX), jnp.bfloat16)
        lay_ref[0, slots] = jnp.zeros((channels, VOX), jnp.bfloat16)
        lay_ref[1, slots] = jnp.zeros((channels, VOX), jnp.bfloat16)
        place = place_ref[...]
        spread = spread_ref[...]
        for k in range(peers):
            first = pl.ds(jnp.bitwise_xor(me_ref[0], k) * blocks, blocks)
            rows = face_refs[k][...].reshape(blocks * channels, 256)
            wide = jnp.dot(rows, place, preferred_element_type=jnp.float32)
            same_ref[first] = wide.astype(jnp.bfloat16).reshape(blocks, channels, VOX)
            rows = layer_refs[k][...].reshape(blocks * channels, 128)
            for t in range(2):
                layer = rows[:, 64 * t:64 * (t + 1)]
                wide = jnp.dot(layer, spread, preferred_element_type=jnp.float32)
                lay_ref[t, first] = wide.astype(jnp.bfloat16).reshape(blocks, channels, VOX)

        gf_ref[...] = jnp.zeros_like(gf_ref)
        acc_ref[...] = jnp.zeros_like(acc_ref)

        def body(s, carry):
            def own(k):
                return g_ref[s, :, 128 * k:128 * (k + 1)]

            def neighbour(e, k):
                q = jnp.minimum(nbr_ref[s, NEIGHBOURS.index(e)], slots)
                if e[2] == 0:
                    return same_ref[q, :, 128 * k:128 * (k + 1)]
                return lay_ref[0 if e[2] < 0 else 1, q, :, 128 * k:128 * (k + 1)]

            for a in (-1, 0, 1):
                kx = 3 if a > 0 else 0
                mx = half == (1 if a > 0 else 0)
                for b in (-1, 0, 1):
                    my = ycoord == (7 if b > 0 else 0)
                    flat = []
                    for k in range(4):
                        f = own(k)
                        if a != 0 and k == kx:
                            f = jnp.where(mx, neighbour((-a, 0, 0), k), f)
                        if b != 0:
                            f = jnp.where(my, neighbour((0, -b, 0), k), f)
                        if a != 0 and b != 0 and k == kx:
                            f = jnp.where(mx & my, neighbour((-a, -b, 0), k), f)
                        flat.append(f)
                    for c in (-1, 0, 1):
                        chunks = []
                        for k in range(4):
                            z = flat[k]
                            if c != 0:
                                y = neighbour((0, 0, -c), k)
                                if a != 0 and k == kx:
                                    y = jnp.where(mx, neighbour((-a, 0, -c), k), y)
                                if b != 0:
                                    y = jnp.where(my, neighbour((0, -b, -c), k), y)
                                if a != 0 and b != 0 and k == kx:
                                    y = jnp.where(mx & my, neighbour((-a, -b, -c), k), y)
                                z = jnp.where(zcoord == (0 if c > 0 else 7), y,
                                              pltpu.roll(z, c % 128, 1))
                            if b != 0:
                                z = jnp.where(ycoord == (0 if b > 0 else 7),
                                              pltpu.roll(z, (-56 * b) % 128, 1),
                                              pltpu.roll(z, (8 * b) % 128, 1))
                            chunks.append(z)
                        if a != 0:
                            turned = [pltpu.roll(z, 64, 1) for z in chunks]
                            keep = half == (1 if a > 0 else 0)
                            chunks = [jnp.where(keep, turned[k], turned[(k - a) % 4]) for k in range(4)]
                        di = 9 * (a + 1) + 3 * (b + 1) + (c + 1)
                        for k in range(4):
                            stack_ref[di * channels:(di + 1) * channels, 128 * k:128 * (k + 1)] = chunks[k]
            st = stack_ref[...]
            gf = jnp.dot(kmix_ref[...], st, preferred_element_type=jnp.float32)
            gf_ref[s] = gf.astype(jnp.bfloat16)
            acc_ref[...] += lax.dot_general(
                f_ref[s], st, (((1,), (1,)), ((), ())), preferred_element_type=jnp.float32
            )
            return carry

        lax.fori_loop(0, jnp.minimum(cnt_ref[0], blocks), body, 0)
        half_rows = channels // 2
        core = me_ref[0] % 2
        keep_ref[...] = acc_ref[pl.ds(pl.multiple_of(core * half_rows, half_rows), half_rows), :] * scaling
        send_ref[...] = (
            acc_ref[pl.ds(pl.multiple_of((1 - core) * half_rows, half_rows), half_rows), :] * scaling
        )

    return kernel


def local_conv(neighbours, block_count, me, grad_out, features, kmix, place, spread, shared, scaling):
    blocks, channels = grad_out.shape[0], grad_out.shape[1]
    peers = len(shared) // 2
    slots = blocks * peers
    smem = pl.BlockSpec(memory_space=pltpu.SMEM)
    vmem = pl.BlockSpec(memory_space=pltpu.VMEM)
    return pl.pallas_call(
        make_kernel(blocks, channels, peers, scaling),
        out_shape=(
            jax.ShapeDtypeStruct((blocks, channels, VOX), jnp.bfloat16),
            jax.ShapeDtypeStruct((channels // 2, 27 * channels), jnp.float32),
            jax.ShapeDtypeStruct((channels // 2, 27 * channels), jnp.float32),
        ),
        in_specs=[smem, smem, smem, vmem, vmem, vmem, vmem, vmem] + [vmem] * (2 * peers),
        out_specs=(vmem, vmem, vmem),
        scratch_shapes=[
            pltpu.VMEM((slots + 1, channels, VOX), jnp.bfloat16),
            pltpu.VMEM((2, slots + 1, channels, VOX), jnp.bfloat16),
            pltpu.VMEM((27 * channels, VOX), jnp.bfloat16),
            pltpu.VMEM((channels, 27 * channels), jnp.float32),
        ],
    )(neighbours, block_count, me, grad_out, features, kmix, place, spread, *shared)


def on_device(grad_out, features, kernel, block_count, neighbours):
    blocks, channels = grad_out.shape[0], grad_out.shape[1]
    pick, place, spread = selectors()
    faces, lowest, highest = pack(grad_out, pick)
    peers = lax.axis_size("split") * lax.axis_size("sub")
    assert peers & (peers - 1) == 0

    def spread_in_brick(x):
        return [x] + [
            lax.ppermute(x, ("split", "sub"), [(i, i ^ k) for i in range(peers)])
            for k in range(1, peers)
        ]

    from_below = from_behind(highest, "brick", 1)
    from_above = from_behind(lowest, "brick", -1)
    shared = spread_in_brick(faces) + spread_in_brick(
        jnp.concatenate([from_below, from_above], axis=2)
    )
    me = (lax.axis_index("split") * lax.axis_size("sub") + lax.axis_index("sub")).astype(jnp.int32)
    kmix = jnp.transpose(kernel, (1, 0, 2)).reshape(channels, 27 * channels)
    scaling = 1.0 / math.sqrt(
        lax.axis_size("brick") * lax.axis_size("split") * lax.axis_size("sub") * blocks * VOX
    )
    assert lax.axis_size("sub") == 2
    grad_features, keep, send = local_conv(
        neighbours, block_count, me.reshape(1), grad_out, features, kmix, place, spread,
        shared, scaling,
    )
    pair = [(0, 1), (1, 0)]
    half = xor_group_sum(keep + lax.ppermute(send, "sub", pair), ("brick", "split"), group=2)
    other = lax.ppermute(half, "sub", pair)
    first = lax.axis_index("sub") == 0
    full = jnp.where(first, jnp.concatenate([half, other]), jnp.concatenate([other, half]))
    totals = jnp.transpose(full.reshape(channels, 27, channels), (1, 0, 2))
    return (grad_features, totals)


def solution(mesh):
    placed = (
        P(("groups", "brick", "split", "sub"), None, None),
        P(("groups", "brick", "split", "sub"), None, None),
        P(),
        P(("groups", "brick", "split", "sub")),
        P(("groups", "brick", "split", "sub"), None),
    )
    return jax.shard_map(
        on_device,
        mesh=mesh,
        in_specs=placed,
        out_specs=(P(("groups", "brick", "split", "sub"), None, None), P("groups", None, None)),
        check_vma=False,
    )
```
